256 devices in a mesh: tile: 16 (over z, core), tensor: 16 (over y, x).
Axes of the slice: x: 4, y: 4, z: 8, core: 2. Of those that a mesh axis runs over, the one named last changes fastest.
Arguments:
- image_hidden: bfloat16 [8, 32, 32, 3072], P(None, 'tile', 'tensor'), may hold values from -6 to 6
- text_hidden: bfloat16 [8, 512, 3072], P(None, ('tile', 'tensor')), may hold values from -6 to 6
- latents: float32 [8, 32, 2048], P(None, 'tile', 'tensor'), may hold values from -6 to 6
- step_index: int32 [8], replicated, may hold values from 0 to 27
- anchor: int32 [8, 2], replicated, may hold values from 0 to 63
- text_len: int32 [8], replicated, may hold values from 64 to 512
- mod_image: float32 [8, 3, 3072], replicated, may hold values from -3 to 3
- mod_text: float32 [8, 3, 3072], replicated, may hold values from -3 to 3
- mod_mlp: float32 [8, 3, 3072], replicated, may hold values from -3 to 3
- mod_final: float32 [8, 2, 3072], replicated, may hold values from -3 to 3
- qkv_image: bfloat16 [3072, 3, 2048], P(None, None, 'tensor'), may hold values from -0.109375 to 0.109375
- qkv_text: bfloat16 [3072, 3, 2048], P(None, None, 'tensor'), may hold values from -0.109375 to 0.109375
- proj_image: bfloat16 [2048, 3072], P('tensor'), may hold values from -0.125 to 0.125
- proj_text: bfloat16 [2048, 3072], P('tensor'), may hold values from -0.125 to 0.125
- qk_gain: float32 [2, 2, 128], replicated, may hold values from 0.5 to 10
- mlp_expand: bfloat16 [3072, 6144], P(None, 'tensor'), may hold values from -0.109375 to 0.109375
- mlp_reduce: bfloat16 [6144, 3072], P('tensor'), may hold values from -0.078125 to 0.078125
- final_weight: bfloat16 [3072, 64], replicated, may hold values from -0.109375 to 0.109375
Outputs:
- image_out: bfloat16 [8, 32, 32, 3072], P(None, 'tile', 'tensor')
- text_out: bfloat16 [8, 512, 3072], P(None, ('tile', 'tensor'))
- latents_ext: float32 [8, 64, 2048], P(None, 'tile', 'tensor')
The draws below stay inside these ranges and needn't reach their ends.
Inputs may be any that keep to these rules, and one draw needn't show every extreme that they name: text_len gives each request's live text tokens; slots at or past it take no part as keys. step_index is a step of the 28-step plan.
All inputs are finite; a program needn't handle non-finite values.
Results may differ from the reference program's by a relative error of at most 0.0085.
The reference program's roundings to bfloat16 on the way (of `image_mod`, `text_mod`, `probs`, `attended`, `mlp_mod`, `activated` and `final_in`) count: a program that leaves them out, or rounds other values in their place, can miss the bound.
Values may be sent and summed in bfloat16 or wider, within the bound.
No kernel may reach another device: no remote copies, remote signals or barrier semaphores. Data moves between devices by JAX's collectives and lax.ppermute only.
A program may use at most 128 MiB of HBM per device.

```python
import math
import jax
import jax.numpy as jnp
from jax import lax

D = 3072
HEADS = 16
HEAD_DIM = 128
MLP = 6144
C = 64
GRID = 32
L_TXT = 512
REQS = 8
NSTEPS = 28
N_TILE = 16


def draw_qk_gain(key, part):
    base_key = jax.random.fold_in(key, 0)
    gains = jax.random.uniform(base_key, (2, 2, HEAD_DIM), jnp.float32, 0.5, 3.2)
    return gains


def touch_ends(drawn, key, low, top_value):
    place = [jax.random.randint(jax.random.fold_in(key, axis), (), 0, length) for axis, length in enumerate(drawn.shape)]
    widest = drawn.shape.index(max(drawn.shape))
    beside = place[:widest] + [(place[widest] + 1) % drawn.shape[widest]] + place[widest + 1:]
    return drawn.at[tuple(place)].set(low).at[tuple(beside)].set(top_value)


def steps_of(key, shape, cuts, least, high):
    def one(axis_at, parts):
        draws = jax.random.uniform(jax.random.fold_in(jax.random.fold_in(key, 6), axis_at), (parts,), jnp.float32, least / len(cuts), high / len(cuts))
        return jnp.repeat(jnp.exp(draws), shape[axis_at] // parts).reshape((-1,) + (1,) * (len(shape) - axis_at - 1))

    level = one(*cuts[0])
    for cut in cuts[1:]:
        level = level * one(*cut)
    return level


def normal_values(key, dims, deviation, limit, cuts=(), kind=jnp.bfloat16):
    values = deviation * jax.random.normal(key, dims, jnp.float32)
    if cuts:
        values = values * steps_of(key, dims, cuts, -0.22, 0.18)
    return jnp.clip(values, -limit, limit).astype(kind)


def setup_inputs(seed: int = 0) -> dict:
    key_of = jax.random.split(jax.random.key(seed), 19)
    image_hidden = normal_values(key_of[0], (REQS, GRID, GRID, D), 1.0, 6.0, ((1, 16), (2, 16)))
    text_hidden = normal_values(key_of[1], (REQS, L_TXT, D), 1.0, 6.0, ((1, 256),))
    latents = normal_values(key_of[2], (REQS, GRID, GRID * C), 1.0, 6.0, ((1, 16), (2, 16)), jnp.float32)
    step_index = touch_ends(jax.random.randint(key_of[3], (REQS,), 0, NSTEPS), jax.random.fold_in(key_of[3], 1), 0, NSTEPS - 1).astype(jnp.int32)
    anchor = touch_ends(jax.random.randint(key_of[4], (REQS, 2), 0, 64), jax.random.fold_in(key_of[4], 1), 0, 63).astype(jnp.int32)
    text_len = touch_ends(jax.random.randint(key_of[5], (REQS,), 64, L_TXT + 1), jax.random.fold_in(key_of[5], 1), 64, L_TXT).astype(jnp.int32)
    mod_image = normal_values(key_of[6], (REQS, 3, D), 0.5, 3.0, (), jnp.float32)
    mod_text = normal_values(key_of[7], (REQS, 3, D), 0.5, 3.0, (), jnp.float32)
    mod_mlp = normal_values(key_of[8], (REQS, 3, D), 0.5, 3.0, (), jnp.float32)
    mod_final = normal_values(key_of[9], (REQS, 2, D), 0.5, 3.0, (), jnp.float32)
    qkv_image = normal_values(key_of[10], (D, 3, HEADS * HEAD_DIM), D ** -0.5, 0.109375, ((2, 16),))
    qkv_text = normal_values(key_of[11], (D, 3, HEADS * HEAD_DIM), D ** -0.5, 0.109375, ((2, 16),))
    proj_image = normal_values(key_of[12], (HEADS * HEAD_DIM, D), (HEADS * HEAD_DIM) ** -0.5, 0.125, ((0, 16),))
    proj_text = normal_values(key_of[13], (HEADS * HEAD_DIM, D), (HEADS * HEAD_DIM) ** -0.5, 0.125, ((0, 16),))
    qk_gain = draw_qk_gain(jax.random.fold_in(key_of[18], 71), 0)
    mlp_expand = normal_values(key_of[15], (D, MLP), D ** -0.5, 0.109375, ((1, 16),))
    mlp_reduce = normal_values(key_of[16], (MLP, D), MLP ** -0.5, 0.078125, ((0, 16),))
    final_weight = normal_values(key_of[17], (D, C), D ** -0.5, 0.109375)
    return {"image_hidden": image_hidden, "text_hidden": text_hidden, "latents": latents, "step_index": step_index, "anchor": anchor, "text_len": text_len, "mod_image": mod_image, "mod_text": mod_text, "mod_mlp": mod_mlp, "mod_final": mod_final, "qkv_image": qkv_image, "qkv_text": qkv_text, "proj_image": proj_image, "proj_text": proj_text, "qk_gain": qk_gain, "mlp_expand": mlp_expand, "mlp_reduce": mlp_reduce, "final_weight": final_weight}


norm_eps = 1e-06
time_shift = 3.0

def layer_norm(values):
    average = lax.optimization_barrier(jnp.mean(values, -1, keepdims=True))
    centred = values - average
    spread = lax.optimization_barrier(jnp.mean(centred * centred, -1, keepdims=True))
    return centred * lax.rsqrt(spread + norm_eps)

def modulate(hidden, shift, stretch):
    normed = layer_norm(hidden.astype(jnp.float32))
    return ((1.0 + stretch) * normed + shift).astype(jnp.bfloat16)

def rope_tables(row_ids, col_ids):
    pair_index = jnp.arange(64, dtype=jnp.int32)
    row_rank = (pair_index - 8).astype(jnp.float32)
    col_rank = (pair_index - 36).astype(jnp.float32)
    log_base = math.log(10000.0)
    row_freq = jnp.where((pair_index >= 8) & (pair_index < 36), jnp.exp(-2.0 * row_rank / 56.0 * log_base), 0.0).astype(jnp.float32)
    col_freq = jnp.where(pair_index >= 36, jnp.exp(-2.0 * col_rank / 56.0 * log_base), 0.0).astype(jnp.float32)
    angles = row_ids[..., None] * row_freq + col_ids[..., None] * col_freq
    angles = jnp.repeat(angles, 2, axis=-1)
    sign_table = jnp.where(jnp.arange(128, dtype=jnp.int32) % 2 == 0, -1.0, 1.0).astype(jnp.float32)
    return (jnp.cos(angles), jnp.sin(angles) * sign_table)

def rotate(values, cos_table, sin_table):
    paired = values.reshape(values.shape[:-1] + (values.shape[-1] // 2, 2))
    swapped = jnp.flip(paired, -1).reshape(values.shape)
    return values * cos_table + swapped * sin_table

def head_norm(projected, head_gain):
    squares = lax.optimization_barrier(jnp.mean(projected * projected, -1, keepdims=True))
    return projected * lax.rsqrt(squares + norm_eps) * head_gain

def sigma_of(step_float):
    level = 1.0 - step_float / NSTEPS
    return time_shift * level / (1.0 + (time_shift - 1.0) * level)

def reference(image_hidden, text_hidden, latents, step_index, anchor, text_len, mod_image, mod_text, mod_mlp, mod_final, qkv_image, qkv_text, proj_image, proj_text, qk_gain, mlp_expand, mlp_reduce, final_weight):
    requests = image_hidden.shape[0]
    model_width = image_hidden.shape[3]
    image_count = GRID * GRID
    image_mod = modulate(image_hidden, mod_image[:, 0, None, None, :], mod_image[:, 1, None, None, :]).reshape(requests * image_count, model_width)
    text_mod = modulate(text_hidden, mod_text[:, 0, None, :], mod_text[:, 1, None, :]).reshape(requests * L_TXT, model_width)
    token_index = jnp.arange(image_count, dtype=jnp.int32)
    row_ids = (anchor[:, 0:1] + token_index[None, :] // GRID).astype(jnp.float32)
    col_ids = (anchor[:, 1:2] + token_index[None, :] % GRID).astype(jnp.float32)
    cos_table, sin_table = rope_tables(row_ids, col_ids)
    key_pos = jnp.arange(L_TXT + image_count, dtype=jnp.int32)
    usable = jnp.logical_or(key_pos[None, :] >= L_TXT, key_pos[None, :] < text_len[:, None])
    score_scale = 1.0 / math.sqrt(HEAD_DIM)
    image_heads = qkv_image.reshape(model_width, 3, HEADS, HEAD_DIM).transpose(2, 0, 1, 3).reshape(HEADS, model_width, 3 * HEAD_DIM)
    text_heads = qkv_text.reshape(model_width, 3, HEADS, HEAD_DIM).transpose(2, 0, 1, 3).reshape(HEADS, model_width, 3 * HEAD_DIM)
    image_projs = proj_image.reshape(HEADS, HEAD_DIM, model_width)
    text_projs = proj_text.reshape(HEADS, HEAD_DIM, model_width)

    def one_head(sums, weights):
        image_sum, text_sum = sums
        image_w, text_w, image_p, text_p = weights
        image_qkv = jnp.dot(image_mod, image_w, preferred_element_type=jnp.float32).reshape(requests, image_count, 3, HEAD_DIM)
        text_qkv = jnp.dot(text_mod, text_w, preferred_element_type=jnp.float32).reshape(requests, L_TXT, 3, HEAD_DIM)
        query = jnp.concatenate([head_norm(text_qkv[:, :, 0], qk_gain[1, 0]).astype(jnp.bfloat16), rotate(head_norm(image_qkv[:, :, 0], qk_gain[0, 0]), cos_table, sin_table).astype(jnp.bfloat16)], 1)
        keys = jnp.concatenate([head_norm(text_qkv[:, :, 1], qk_gain[1, 1]).astype(jnp.bfloat16), rotate(head_norm(image_qkv[:, :, 1], qk_gain[0, 1]), cos_table, sin_table).astype(jnp.bfloat16)], 1)
        values = jnp.concatenate([text_qkv[:, :, 2], image_qkv[:, :, 2]], 1).astype(jnp.bfloat16)
        scores = jnp.einsum('rqd,rkd->rqk', query.astype(jnp.float32), keys.astype(jnp.float32)) * score_scale
        masked = jnp.where(usable[:, None, :], scores, -jnp.inf)
        row_top = lax.optimization_barrier(jnp.max(masked, -1, keepdims=True))
        weights_raw = jnp.where(usable[:, None, :], jnp.exp(scores - row_top), 0.0)
        weight_sum = lax.optimization_barrier(jnp.sum(weights_raw, -1, keepdims=True))
        probs = weights_raw.astype(jnp.bfloat16)
        attended = (jnp.einsum('rqk,rkd->rqd', probs.astype(jnp.float32), values.astype(jnp.float32)) / weight_sum).astype(jnp.bfloat16)
        text_sum = text_sum + jnp.dot(attended[:, :L_TXT].reshape(requests * L_TXT, HEAD_DIM), text_p, preferred_element_type=jnp.float32)
        image_sum = image_sum + jnp.dot(attended[:, L_TXT:].reshape(requests * image_count, HEAD_DIM), image_p, preferred_element_type=jnp.float32)
        return ((image_sum, text_sum), None)
    start_sums = (jnp.zeros((requests * image_count, model_width), jnp.float32), jnp.zeros((requests * L_TXT, model_width), jnp.float32))
    (image_sum, text_sum), unused = lax.scan(one_head, start_sums, (image_heads, text_heads, image_projs, text_projs))
    image_mid = (image_hidden.astype(jnp.float32) + mod_image[:, 2, None, None, :] * image_sum.reshape(requests, GRID, GRID, model_width)).astype(jnp.bfloat16)
    text_out = (text_hidden.astype(jnp.float32) + mod_text[:, 2, None, :] * text_sum.reshape(requests, L_TXT, model_width)).astype(jnp.bfloat16)
    mlp_mod = modulate(image_mid, mod_mlp[:, 0, None, None, :], mod_mlp[:, 1, None, None, :]).reshape(requests * image_count, model_width)
    activated = jax.nn.gelu(jnp.dot(mlp_mod, mlp_expand, preferred_element_type=jnp.float32), approximate=True).astype(jnp.bfloat16)
    mlp_sum = jnp.dot(activated, mlp_reduce, preferred_element_type=jnp.float32).reshape(requests, GRID, GRID, model_width)
    image_out = (image_mid.astype(jnp.float32) + mod_mlp[:, 2, None, None, :] * mlp_sum).astype(jnp.bfloat16)
    final_in = modulate(image_out, mod_final[:, 0, None, None, :], mod_final[:, 1, None, None, :])
    velocity = jnp.dot(final_in.reshape(requests * image_count, model_width), final_weight, preferred_element_type=jnp.float32).reshape(requests, GRID, GRID * C)
    step_float = step_index.astype(jnp.float32)
    time_delta = sigma_of(step_float + 1.0) - sigma_of(step_float)
    latents_next = latents + time_delta[:, None, None] * velocity
    padded = jnp.pad(latents_next, ((0, 0), (1, 1), (0, 0)))
    tile_rows = GRID // N_TILE
    row_pick = (jnp.arange(N_TILE, dtype=jnp.int32)[:, None] * tile_rows + jnp.arange(tile_rows + 2, dtype=jnp.int32)[None, :]).reshape(-1)
    latents_ext = padded[:, row_pick, :]
    return (image_out, text_out, latents_ext)
```

```python
import math

import jax
import jax.numpy as jnp
from jax import lax
from jax.sharding import PartitionSpec as P

HEAD_DIM = 128
GRID = 32
NSTEPS = 28


norm_eps = 1e-06
time_shift = 3.0


def padded(value, sides, width):
    for axis, dim in sides:
        size, length = (lax.axis_size(axis), value.shape[dim])
        up = [(i, (i + 1) % size) for i in range(size - 1)]
        down = [(j, i) for i, j in up]
        last = lax.slice_in_dim(value, length - width, length, axis=dim)
        leading = lax.slice_in_dim(value, 0, width, axis=dim)
        before = lax.ppermute(last, axis, up)
        after = lax.ppermute(leading, axis, down)
        value = jnp.concatenate([before, value, after], axis=dim)
    return value


def layer_norm(values):
    average = jnp.mean(values, -1, keepdims=True)
    centred = values - average
    spread = jnp.mean(centred * centred, -1, keepdims=True)
    return centred * lax.rsqrt(spread + norm_eps)


def modulate(hidden, shift, stretch):
    normed = layer_norm(hidden.astype(jnp.float32))
    return ((1.0 + stretch) * normed + shift).astype(jnp.bfloat16)


def rope_tables(row_ids, col_ids):
    pair_index = jnp.arange(64, dtype=jnp.int32)
    row_rank = (pair_index - 8).astype(jnp.float32)
    col_rank = (pair_index - 36).astype(jnp.float32)
    log_base = math.log(10000.0)
    row_freq = jnp.where(
        (pair_index >= 8) & (pair_index < 36), jnp.exp(-2.0 * row_rank / 56.0 * log_base), 0.0
    )
    col_freq = jnp.where(pair_index >= 36, jnp.exp(-2.0 * col_rank / 56.0 * log_base), 0.0)
    angles = row_ids[..., None] * row_freq + col_ids[..., None] * col_freq
    angles = jnp.repeat(angles, 2, axis=-1)
    sign_table = jnp.where(jnp.arange(128, dtype=jnp.int32) % 2 == 0, -1.0, 1.0).astype(jnp.float32)
    return (jnp.cos(angles), jnp.sin(angles) * sign_table)


def rotate(values, cos_table, sin_table):
    paired = values.reshape(values.shape[:-1] + (values.shape[-1] // 2, 2))
    swapped = jnp.flip(paired, -1).reshape(values.shape)
    return values * cos_table + swapped * sin_table


def head_norm(projected, head_gain):
    squares = jnp.mean(projected * projected, -1, keepdims=True)
    return projected * lax.rsqrt(squares + norm_eps) * head_gain


def sigma_of(step_float):
    level = 1.0 - step_float / NSTEPS
    return time_shift * level / (1.0 + (time_shift - 1.0) * level)


def key_usable(text_len, key_count, text_tile, block_len):
    key_pos = jnp.arange(key_count, dtype=jnp.int32)
    owner_tile = key_pos // block_len
    offset = key_pos % block_len
    text_pos = owner_tile * text_tile + offset
    return jnp.logical_or(offset[None, :] >= text_tile, text_pos[None, :] < text_len[:, None])


def per_device(
    image_hidden,
    text_hidden,
    latents,
    step_index,
    anchor,
    text_len,
    mod_image,
    mod_text,
    mod_mlp,
    mod_final,
    qkv_image,
    qkv_text,
    proj_image,
    proj_text,
    qk_gain,
    mlp_expand,
    mlp_reduce,
    final_weight,
):
    requests, tile_rows, tile_cols, model_width = image_hidden.shape
    local_cols = qkv_image.shape[2]
    local_heads = local_cols // HEAD_DIM
    local_units = mlp_expand.shape[1]
    owners = lax.axis_size("tensor")
    own_image = tile_rows * tile_cols
    own_text = text_hidden.shape[1]
    joined = jnp.concatenate(
        [image_hidden.reshape(requests, own_image, model_width), text_hidden], 1
    )
    gathered = lax.all_gather(joined, "tensor", axis=1, tiled=True).reshape(
        requests, owners, own_image + own_text, model_width
    )
    image_all = gathered[:, :, :own_image].reshape(requests, owners * own_image, model_width)
    text_all = gathered[:, :, own_image:].reshape(requests, owners * own_text, model_width)
    image_mod = modulate(image_all, mod_image[:, 0, None, :], mod_image[:, 1, None, :])
    text_mod = modulate(text_all, mod_text[:, 0, None, :], mod_text[:, 1, None, :])
    text_tile = text_mod.shape[1]
    image_count = image_mod.shape[1]
    block_len = text_tile + image_count
    tile_index = lax.axis_index("tile")
    token_index = jnp.arange(image_count, dtype=jnp.int32)
    owner = token_index // own_image
    within = token_index % own_image
    row_ids = (anchor[:, 0:1] + tile_index * tile_rows + within[None, :] // tile_cols).astype(
        jnp.float32
    )
    col_ids = (anchor[:, 1:2] + owner[None, :] * tile_cols + within[None, :] % tile_cols).astype(
        jnp.float32
    )
    cos_table, sin_table = rope_tables(row_ids, col_ids)
    cos_table = cos_table[:, :, None, :]
    sin_table = sin_table[:, :, None, :]
    image_qkv = jnp.dot(
        image_mod.reshape(requests * image_count, model_width),
        qkv_image.reshape(model_width, 3 * local_cols),
        preferred_element_type=jnp.float32,
    ).reshape(requests, image_count, 3, local_heads, HEAD_DIM)
    text_qkv = jnp.dot(
        text_mod.reshape(requests * text_tile, model_width),
        qkv_text.reshape(model_width, 3 * local_cols),
        preferred_element_type=jnp.float32,
    ).reshape(requests, text_tile, 3, local_heads, HEAD_DIM)
    query = jnp.concatenate(
        [
            head_norm(text_qkv[:, :, 0], qk_gain[1, 0]).astype(jnp.bfloat16),
            rotate(head_norm(image_qkv[:, :, 0], qk_gain[0, 0]), cos_table, sin_table).astype(
                jnp.bfloat16
            ),
        ],
        1,
    )
    keys = jnp.concatenate(
        [
            head_norm(text_qkv[:, :, 1], qk_gain[1, 1]).astype(jnp.bfloat16),
            rotate(head_norm(image_qkv[:, :, 1], qk_gain[0, 1]), cos_table, sin_table).astype(
                jnp.bfloat16
            ),
        ],
        1,
    )
    values = jnp.concatenate([text_qkv[:, :, 2], image_qkv[:, :, 2]], 1).astype(jnp.bfloat16)
    score_scale = 1.0 / math.sqrt(HEAD_DIM)
    kv_all = lax.all_gather(jnp.stack([keys, values], 2), "tile", axis=1, tiled=True)
    keys_all, values_all = kv_all[:, :, 0], kv_all[:, :, 1]
    usable = key_usable(text_len, keys_all.shape[1], text_tile, block_len)[:, None, None, :]
    scores = (
        jnp.einsum("rqhd,rkhd->rhqk", query, keys_all, preferred_element_type=jnp.float32)
        * score_scale
    )
    row_top = jnp.max(jnp.where(usable, scores, -jnp.inf), -1, keepdims=True)
    weights_raw = jnp.where(usable, jnp.exp(scores - row_top), 0.0)
    weight_sum = jnp.sum(weights_raw, -1, keepdims=True)
    accum = jnp.einsum(
        "rhqk,rkhd->rhqd",
        weights_raw.astype(jnp.bfloat16),
        values_all,
        preferred_element_type=jnp.float32,
    )
    attended = (accum / weight_sum).transpose(0, 2, 1, 3).astype(jnp.bfloat16)
    text_term = jnp.dot(
        attended[:, :text_tile].reshape(requests * text_tile, local_cols),
        proj_text,
        preferred_element_type=jnp.float32,
    ).reshape(requests, owners, own_text, model_width)
    image_term = jnp.dot(
        attended[:, text_tile:].reshape(requests * image_count, local_cols),
        proj_image,
        preferred_element_type=jnp.float32,
    ).reshape(requests, owners, own_image, model_width)
    both_term = jnp.concatenate([image_term, text_term], 2).reshape(
        requests, owners * (own_image + own_text), model_width
    )
    both_sum = lax.psum_scatter(both_term, "tensor", scatter_dimension=1, tiled=True)
    image_sum = both_sum[:, :own_image].reshape(requests, tile_rows, tile_cols, model_width)
    text_sum = both_sum[:, own_image:]
    image_gate = mod_image[:, 2, None, None, :]
    image_mid = (image_hidden.astype(jnp.float32) + image_gate * image_sum).astype(jnp.bfloat16)
    mlp_mod = modulate(image_mid, mod_mlp[:, 0, None, None, :], mod_mlp[:, 1, None, None, :])
    piece = lax.all_gather(mlp_mod, "tensor", axis=1, tiled=True)
    grown = jnp.dot(piece.reshape(-1, model_width), mlp_expand, preferred_element_type=jnp.float32)
    activated = jax.nn.gelu(grown, approximate=True).astype(jnp.bfloat16)
    text_out = (text_hidden.astype(jnp.float32) + mod_text[:, 2, None, :] * text_sum).astype(
        jnp.bfloat16
    )
    mlp_term = jnp.dot(
        activated,
        mlp_reduce,
        preferred_element_type=jnp.float32,
    ).reshape(requests, owners * tile_rows, tile_cols, model_width)
    mlp_sum = lax.psum_scatter(mlp_term, "tensor", scatter_dimension=1, tiled=True)
    image_out = (image_mid.astype(jnp.float32) + mod_mlp[:, 2, None, None, :] * mlp_sum).astype(
        jnp.bfloat16
    )
    final_in = modulate(image_out, mod_final[:, 0, None, None, :], mod_final[:, 1, None, None, :])
    velocity = jnp.dot(
        final_in.reshape(requests * tile_rows * tile_cols, model_width),
        final_weight,
        preferred_element_type=jnp.float32,
    ).reshape(requests, tile_rows, tile_cols * final_weight.shape[1])
    step_float = step_index.astype(jnp.float32)
    time_delta = sigma_of(step_float + 1.0) - sigma_of(step_float)
    latents_next = latents + time_delta[:, None, None] * velocity
    latents_ext = padded(latents_next, (("tile", 1),), 1)
    return (image_out, text_out, latents_ext)


def solution(mesh):
    return jax.shard_map(
        per_device,
        mesh=mesh,
        in_specs=(
            P(None, "tile", "tensor", None),
            P(None, ("tile", "tensor"), None),
            P(None, "tile", "tensor"),
            P(),
            P(),
            P(),
            P(),
            P(),
            P(),
            P(),
            P(None, None, "tensor"),
            P(None, None, "tensor"),
            P("tensor", None),
            P("tensor", None),
            P(),
            P(None, "tensor"),
            P("tensor", None),
            P(),
        ),
        out_specs=(
            P(None, "tile", "tensor", None),
            P(None, ("tile", "tensor"), None),
            P(None, "tile", "tensor"),
        ),
        check_vma=False,
    )
```

```python
import math

import jax
import jax.numpy as jnp
from jax import lax
from jax.sharding import PartitionSpec as P

HEAD_DIM = 128
GRID = 32
NSTEPS = 28


norm_eps = 1e-06
time_shift = 3.0


def padded(value, sides, width):
    for axis, dim in sides:
        size, length = (lax.axis_size(axis), value.shape[dim])
        up = [(i, (i + 1) % size) for i in range(size - 1)]
        down = [(j, i) for i, j in up]
        last = lax.slice_in_dim(value, length - width, length, axis=dim)
        leading = lax.slice_in_dim(value, 0, width, axis=dim)
        before = lax.ppermute(last, axis, up)
        after = lax.ppermute(leading, axis, down)
        value = jnp.concatenate([before, value, after], axis=dim)
    return value


def layer_norm(values):
    average = jnp.mean(values, -1, keepdims=True)
    centred = values - average
    spread = jnp.mean(centred * centred, -1, keepdims=True)
    return centred * lax.rsqrt(spread + norm_eps)


def modulate(hidden, shift, stretch):
    normed = layer_norm(hidden.astype(jnp.float32))
    return ((1.0 + stretch) * normed + shift).astype(jnp.bfloat16)


def rope_tables(row_ids, col_ids):
    lane = jnp.arange(2 * 64, dtype=jnp.int32)
    pair_index = lane // 2
    row_rank = (pair_index - 8).astype(jnp.float32)
    col_rank = (pair_index - 36).astype(jnp.float32)
    log_base = math.log(10000.0)
    row_freq = jnp.where(
        (pair_index >= 8) & (pair_index < 36), jnp.exp(-2.0 * row_rank / 56.0 * log_base), 0.0
    )
    col_freq = jnp.where(pair_index >= 36, jnp.exp(-2.0 * col_rank / 56.0 * log_base), 0.0)
    angles = row_ids[..., None] * row_freq + col_ids[..., None] * col_freq
    sign_table = jnp.where(lane % 2 == 0, -1.0, 1.0).astype(jnp.float32)
    return (jnp.cos(angles), jnp.sin(angles) * sign_table)


def rotate(values, cos_table, sin_table):
    lane = lax.broadcasted_iota(jnp.int32, values.shape, values.ndim - 1)
    swapped = jnp.where(
        lane % 2 == 0, jnp.roll(values, -1, axis=-1), jnp.roll(values, 1, axis=-1)
    )
    return values * cos_table + swapped * sin_table


def head_norm(projected, head_gain):
    squares = jnp.mean(projected * projected, -1, keepdims=True)
    return projected * lax.rsqrt(squares + norm_eps) * head_gain


def sigma_of(step_float):
    level = 1.0 - step_float / NSTEPS
    return time_shift * level / (1.0 + (time_shift - 1.0) * level)


def key_usable(text_len, key_count, text_tile, block_len):
    key_pos = jnp.arange(key_count, dtype=jnp.int32)
    owner_tile = key_pos // block_len
    offset = key_pos % block_len
    text_pos = owner_tile * text_tile + offset
    return jnp.logical_or(offset[None, :] >= text_tile, text_pos[None, :] < text_len[:, None])


def per_device(
    image_hidden,
    text_hidden,
    latents,
    step_index,
    anchor,
    text_len,
    mod_image,
    mod_text,
    mod_mlp,
    mod_final,
    qkv_image,
    qkv_text,
    proj_image,
    proj_text,
    qk_gain,
    mlp_expand,
    mlp_reduce,
    final_weight,
):
    requests, tile_rows, tile_cols, model_width = image_hidden.shape
    local_cols = qkv_image.shape[2]
    local_heads = local_cols // HEAD_DIM
    local_units = mlp_expand.shape[1]
    owners = lax.axis_size("tensor")
    own_image = tile_rows * tile_cols
    own_text = text_hidden.shape[1]
    image_mod_own = modulate(
        image_hidden.reshape(requests, own_image, model_width),
        mod_image[:, 0, None, :],
        mod_image[:, 1, None, :],
    )
    text_mod_own = modulate(text_hidden, mod_text[:, 0, None, :], mod_text[:, 1, None, :])
    joined = jnp.concatenate([image_mod_own, text_mod_own], 1)
    gathered = lax.all_gather(joined, "tensor", axis=1, tiled=True).reshape(
        requests, owners, own_image + own_text, model_width
    )
    image_mod = gathered[:, :, :own_image].reshape(requests, owners * own_image, model_width)
    text_mod = gathered[:, :, own_image:].reshape(requests, owners * own_text, model_width)
    text_tile = text_mod.shape[1]
    image_count = image_mod.shape[1]
    block_len = text_tile + image_count
    tile_index = lax.axis_index("tile")
    token_index = jnp.arange(image_count, dtype=jnp.int32)
    owner = token_index // own_image
    within = token_index % own_image
    row_ids = (anchor[:, 0:1] + tile_index * tile_rows + within[None, :] // tile_cols).astype(
        jnp.float32
    )
    col_ids = (anchor[:, 1:2] + owner[None, :] * tile_cols + within[None, :] % tile_cols).astype(
        jnp.float32
    )
    cos_table, sin_table = rope_tables(row_ids, col_ids)
    cos_table = cos_table[:, :, None, :]
    sin_table = sin_table[:, :, None, :]
    image_qkv = jnp.dot(
        image_mod.reshape(requests * image_count, model_width),
        qkv_image.reshape(model_width, 3 * local_cols),
        preferred_element_type=jnp.float32,
    ).reshape(requests, image_count, 3, local_heads, HEAD_DIM)
    text_qkv = jnp.dot(
        text_mod.reshape(requests * text_tile, model_width),
        qkv_text.reshape(model_width, 3 * local_cols),
        preferred_element_type=jnp.float32,
    ).reshape(requests, text_tile, 3, local_heads, HEAD_DIM)
    query = jnp.concatenate(
        [
            head_norm(text_qkv[:, :, 0], qk_gain[1, 0]).astype(jnp.bfloat16),
            rotate(head_norm(image_qkv[:, :, 0], qk_gain[0, 0]), cos_table, sin_table).astype(
                jnp.bfloat16
            ),
        ],
        1,
    )
    keys = jnp.concatenate(
        [
            head_norm(text_qkv[:, :, 1], qk_gain[1, 1]).astype(jnp.bfloat16),
            rotate(head_norm(image_qkv[:, :, 1], qk_gain[0, 1]), cos_table, sin_table).astype(
                jnp.bfloat16
            ),
        ],
        1,
    )
    values = jnp.concatenate([text_qkv[:, :, 2], image_qkv[:, :, 2]], 1).astype(jnp.bfloat16)
    score_scale = 1.0 / math.sqrt(HEAD_DIM)
    kv_all = lax.all_gather(jnp.stack([keys, values], 2), "tile", axis=1, tiled=True)
    keys_all, values_all = kv_all[:, :, 0], kv_all[:, :, 1]
    usable = key_usable(text_len, keys_all.shape[1], text_tile, block_len)[:, None, None, :]
    scores = (
        jnp.einsum("rqhd,rkhd->rhqk", query, keys_all, preferred_element_type=jnp.float32)
        * score_scale
    )
    row_top = jnp.max(jnp.where(usable, scores, -jnp.inf), -1, keepdims=True)
    weights_raw = jnp.where(usable, jnp.exp(scores - row_top), 0.0)
    weight_sum = jnp.sum(weights_raw, -1, keepdims=True)
    accum = jnp.einsum(
        "rhqk,rkhd->rhqd",
        weights_raw.astype(jnp.bfloat16),
        values_all,
        preferred_element_type=jnp.float32,
    )
    attended = (accum / weight_sum).transpose(0, 2, 1, 3).astype(jnp.bfloat16)
    text_att = attended[:, :text_tile].reshape(requests, owners, own_text, local_cols)
    image_att = attended[:, text_tile:].reshape(requests, owners, own_image, local_cols)
    zeros_t = jnp.zeros_like(text_att)
    zeros_i = jnp.zeros_like(image_att)
    stacked = jnp.concatenate(
        [
            jnp.concatenate([image_att, zeros_i], 3),
            jnp.concatenate([zeros_t, text_att], 3),
        ],
        2,
    ).reshape(requests * owners * (own_image + own_text), 2 * local_cols)
    both_proj = jnp.concatenate([proj_image, proj_text], 0)
    both_term = jnp.dot(stacked, both_proj, preferred_element_type=jnp.float32).reshape(
        requests, owners * (own_image + own_text), model_width
    )
    both_sum = lax.psum_scatter(both_term, "tensor", scatter_dimension=1, tiled=True)
    image_sum = both_sum[:, :own_image].reshape(requests, tile_rows, tile_cols, model_width)
    text_sum = both_sum[:, own_image:]
    image_gate = mod_image[:, 2, None, None, :]
    image_mid = (image_hidden.astype(jnp.float32) + image_gate * image_sum).astype(jnp.bfloat16)
    mlp_mod = modulate(image_mid, mod_mlp[:, 0, None, None, :], mod_mlp[:, 1, None, None, :])
    piece = lax.all_gather(
        mlp_mod.reshape(requests, own_image, model_width), "tensor", axis=1, tiled=True
    )
    grown = jnp.dot(piece.reshape(-1, model_width), mlp_expand, preferred_element_type=jnp.float32)
    activated = jax.nn.gelu(grown, approximate=True).astype(jnp.bfloat16)
    text_out = (text_hidden.astype(jnp.float32) + mod_text[:, 2, None, :] * text_sum).astype(
        jnp.bfloat16
    )
    mlp_term = jnp.dot(
        activated,
        mlp_reduce,
        preferred_element_type=jnp.float32,
    ).reshape(requests, owners * own_image, model_width)
    mlp_sum = lax.psum_scatter(mlp_term, "tensor", scatter_dimension=1, tiled=True).reshape(
        requests, tile_rows, tile_cols, model_width
    )
    image_out = (image_mid.astype(jnp.float32) + mod_mlp[:, 2, None, None, :] * mlp_sum).astype(
        jnp.bfloat16
    )
    final_in = modulate(image_out, mod_final[:, 0, None, None, :], mod_final[:, 1, None, None, :])
    velocity = jnp.dot(
        final_in.reshape(requests * tile_rows * tile_cols, model_width),
        final_weight,
        preferred_element_type=jnp.float32,
    ).reshape(requests, tile_rows, tile_cols * final_weight.shape[1])
    step_float = step_index.astype(jnp.float32)
    time_delta = sigma_of(step_float + 1.0) - sigma_of(step_float)
    latents_next = latents + time_delta[:, None, None] * velocity
    latents_ext = padded(latents_next, (("tile", 1),), 1)
    return (image_out, text_out, latents_ext)


def solution(mesh):
    return jax.shard_map(
        per_device,
        mesh=mesh,
        in_specs=(
            P(None, "tile", "tensor", None),
            P(None, ("tile", "tensor"), None),
            P(None, "tile", "tensor"),
            P(),
            P(),
            P(),
            P(),
            P(),
            P(),
            P(),
            P(None, None, "tensor"),
            P(None, None, "tensor"),
            P("tensor", None),
            P("tensor", None),
            P(),
            P(None, "tensor"),
            P("tensor", None),
            P(),
        ),
        out_specs=(
            P(None, "tile", "tensor", None),
            P(None, ("tile", "tensor"), None),
            P(None, "tile", "tensor"),
        ),
        check_vma=False,
    )
```

```python
import math

import jax
import jax.numpy as jnp
from jax import lax
from jax.sharding import PartitionSpec as P

HEAD_DIM = 128
GRID = 32
NSTEPS = 28


norm_eps = 1e-06
time_shift = 3.0


def padded(value, sides, width):
    for axis, dim in sides:
        size, length = (lax.axis_size(axis), value.shape[dim])
        up = [(i, (i + 1) % size) for i in range(size - 1)]
        down = [(j, i) for i, j in up]
        last = lax.slice_in_dim(value, length - width, length, axis=dim)
        leading = lax.slice_in_dim(value, 0, width, axis=dim)
        before = lax.ppermute(last, axis, up)
        after = lax.ppermute(leading, axis, down)
        value = jnp.concatenate([before, value, after], axis=dim)
    return value


def layer_norm(values):
    average = jnp.mean(values, -1, keepdims=True)
    centred = values - average
    spread = jnp.mean(centred * centred, -1, keepdims=True)
    return centred * lax.rsqrt(spread + norm_eps)


def modulate(hidden, shift, stretch):
    normed = layer_norm(hidden.astype(jnp.float32))
    return ((1.0 + stretch) * normed + shift).astype(jnp.bfloat16)


def rope_tables(row_ids, col_ids):
    lane = jnp.arange(2 * 64, dtype=jnp.int32)
    pair_index = lane // 2
    row_rank = (pair_index - 8).astype(jnp.float32)
    col_rank = (pair_index - 36).astype(jnp.float32)
    log_base = math.log(10000.0)
    row_freq = jnp.where(
        (pair_index >= 8) & (pair_index < 36), jnp.exp(-2.0 * row_rank / 56.0 * log_base), 0.0
    )
    col_freq = jnp.where(pair_index >= 36, jnp.exp(-2.0 * col_rank / 56.0 * log_base), 0.0)
    angles = row_ids[..., None] * row_freq + col_ids[..., None] * col_freq
    sign_table = jnp.where(lane % 2 == 0, -1.0, 1.0).astype(jnp.float32)
    return (jnp.cos(angles), jnp.sin(angles) * sign_table)


def rotate(values, cos_table, sin_table):
    lane = lax.broadcasted_iota(jnp.int32, values.shape, values.ndim - 1)
    swapped = jnp.where(
        lane % 2 == 0, jnp.roll(values, -1, axis=-1), jnp.roll(values, 1, axis=-1)
    )
    return values * cos_table + swapped * sin_table


def head_norm(projected, head_gain):
    squares = jnp.mean(projected * projected, -1, keepdims=True)
    return projected * lax.rsqrt(squares + norm_eps) * head_gain


def sigma_of(step_float):
    level = 1.0 - step_float / NSTEPS
    return time_shift * level / (1.0 + (time_shift - 1.0) * level)


def key_usable(text_len, key_count, text_tile, block_len):
    key_pos = jnp.arange(key_count, dtype=jnp.int32)
    owner_tile = key_pos // block_len
    offset = key_pos % block_len
    text_pos = owner_tile * text_tile + offset
    return jnp.logical_or(offset[None, :] >= text_tile, text_pos[None, :] < text_len[:, None])


def sum_over_tensor(term, owners, narrow):
    if not narrow:
        return lax.psum_scatter(term, "tensor", scatter_dimension=0, tiled=True)
    parts = term.astype(jnp.bfloat16).reshape((owners, -1) + term.shape[1:])
    parts = lax.all_to_all(parts, "tensor", 0, 0, tiled=True)
    return jnp.sum(parts.astype(jnp.float32), 0)


NARROW_SUMS = True


def per_device(
    image_hidden,
    text_hidden,
    latents,
    step_index,
    anchor,
    text_len,
    mod_image,
    mod_text,
    mod_mlp,
    mod_final,
    qkv_image,
    qkv_text,
    proj_image,
    proj_text,
    qk_gain,
    mlp_expand,
    mlp_reduce,
    final_weight,
):
    requests, tile_rows, tile_cols, model_width = image_hidden.shape
    local_cols = qkv_image.shape[2]
    local_heads = local_cols // HEAD_DIM
    owners = lax.axis_size("tensor")
    own_image = tile_rows * tile_cols
    own_text = text_hidden.shape[1]
    slots = own_image + own_text
    image_own = image_hidden.reshape(requests, own_image, model_width).transpose(1, 0, 2)
    text_own = text_hidden.transpose(1, 0, 2)
    image_mod_own = modulate(image_own, mod_image[None, :, 0, :], mod_image[None, :, 1, :])
    text_mod_own = modulate(text_own, mod_text[None, :, 0, :], mod_text[None, :, 1, :])
    joined = jnp.concatenate([image_mod_own, text_mod_own], 0)
    gathered = lax.all_gather(joined, "tensor", axis=0, tiled=True).reshape(
        owners, slots, requests, model_width
    )
    image_count = owners * own_image
    text_tile = owners * own_text
    block_len = text_tile + image_count
    image_mod = gathered[:, :own_image].reshape(image_count * requests, model_width)
    text_mod = gathered[:, own_image:].reshape(text_tile * requests, model_width)
    tile_index = lax.axis_index("tile")
    token_index = jnp.arange(image_count, dtype=jnp.int32)
    owner = token_index // own_image
    within = token_index % own_image
    row_ids = (anchor[None, :, 0] + tile_index * tile_rows + (within // tile_cols)[:, None]).astype(
        jnp.float32
    )
    col_ids = (anchor[None, :, 1] + (owner * tile_cols + within % tile_cols)[:, None]).astype(
        jnp.float32
    )
    cos_table, sin_table = rope_tables(row_ids, col_ids)
    cos_table = cos_table[:, :, None, :]
    sin_table = sin_table[:, :, None, :]
    image_qkv = jnp.dot(
        image_mod, qkv_image.reshape(model_width, 3 * local_cols), preferred_element_type=jnp.float32
    ).reshape(image_count, requests, 3, local_heads, HEAD_DIM)
    text_qkv = jnp.dot(
        text_mod, qkv_text.reshape(model_width, 3 * local_cols), preferred_element_type=jnp.float32
    ).reshape(text_tile, requests, 3, local_heads, HEAD_DIM)
    query = jnp.concatenate(
        [
            head_norm(text_qkv[:, :, 0], qk_gain[1, 0]).astype(jnp.bfloat16),
            rotate(head_norm(image_qkv[:, :, 0], qk_gain[0, 0]), cos_table, sin_table).astype(
                jnp.bfloat16
            ),
        ],
        0,
    )
    keys = jnp.concatenate(
        [
            head_norm(text_qkv[:, :, 1], qk_gain[1, 1]).astype(jnp.bfloat16),
            rotate(head_norm(image_qkv[:, :, 1], qk_gain[0, 1]), cos_table, sin_table).astype(
                jnp.bfloat16
            ),
        ],
        0,
    )
    values = jnp.concatenate([text_qkv[:, :, 2], image_qkv[:, :, 2]], 0).astype(jnp.bfloat16)
    score_scale = 1.0 / math.sqrt(HEAD_DIM)
    kv_all = lax.all_gather(jnp.stack([keys, values], 1), "tile", axis=0, tiled=True)
    keys_all, values_all = kv_all[:, 0], kv_all[:, 1]
    usable = key_usable(text_len, keys_all.shape[0], text_tile, block_len)[:, None, None, :]
    scores = (
        jnp.einsum("qrhd,krhd->rhqk", query, keys_all, preferred_element_type=jnp.float32)
        * score_scale
    )
    row_top = jnp.max(jnp.where(usable, scores, -jnp.inf), -1, keepdims=True)
    weights_raw = jnp.where(usable, jnp.exp(scores - row_top), 0.0)
    weight_sum = jnp.sum(weights_raw, -1, keepdims=True)
    accum = jnp.einsum(
        "rhqk,krhd->rhqd",
        weights_raw.astype(jnp.bfloat16),
        values_all,
        preferred_element_type=jnp.float32,
    )
    attended = (
        (accum / weight_sum).astype(jnp.bfloat16).transpose(2, 0, 1, 3).reshape(
            block_len, requests, local_cols
        )
    )
    text_att = attended[:text_tile].reshape(owners, own_text, requests, local_cols)
    image_att = attended[text_tile:].reshape(owners, own_image, requests, local_cols)
    stacked = jnp.concatenate(
        [
            jnp.concatenate([image_att, jnp.zeros_like(image_att)], 3),
            jnp.concatenate([jnp.zeros_like(text_att), text_att], 3),
        ],
        1,
    ).reshape(owners * slots * requests, 2 * local_cols)
    both_proj = jnp.concatenate([proj_image, proj_text], 0)
    both_term = jnp.dot(stacked, both_proj, preferred_element_type=jnp.float32).reshape(
        owners * slots, requests, model_width
    )
    both_sum = sum_over_tensor(both_term, owners, NARROW_SUMS)
    image_sum = both_sum[:own_image]
    text_sum = both_sum[own_image:]
    image_mid = (image_own.astype(jnp.float32) + mod_image[None, :, 2, :] * image_sum).astype(
        jnp.bfloat16
    )
    mlp_mod = modulate(image_mid, mod_mlp[None, :, 0, :], mod_mlp[None, :, 1, :])
    piece = lax.all_gather(mlp_mod, "tensor", axis=0, tiled=True)
    grown = jnp.dot(piece.reshape(-1, model_width), mlp_expand, preferred_element_type=jnp.float32)
    activated = jax.nn.gelu(grown, approximate=True).astype(jnp.bfloat16)
    text_out = (text_own.astype(jnp.float32) + mod_text[None, :, 2, :] * text_sum).astype(
        jnp.bfloat16
    )
    mlp_term = jnp.dot(activated, mlp_reduce, preferred_element_type=jnp.float32).reshape(
        image_count, requests, model_width
    )
    mlp_sum = sum_over_tensor(mlp_term, owners, NARROW_SUMS)
    image_out = (image_mid.astype(jnp.float32) + mod_mlp[None, :, 2, :] * mlp_sum).astype(
        jnp.bfloat16
    )
    final_in = modulate(image_out, mod_final[None, :, 0, :], mod_final[None, :, 1, :])
    velocity = jnp.dot(
        final_in.reshape(own_image * requests, model_width),
        final_weight,
        preferred_element_type=jnp.float32,
    ).reshape(own_image, requests, final_weight.shape[1])
    velocity = velocity.transpose(1, 0, 2).reshape(
        requests, tile_rows, tile_cols * final_weight.shape[1]
    )
    step_float = step_index.astype(jnp.float32)
    time_delta = sigma_of(step_float + 1.0) - sigma_of(step_float)
    latents_next = latents + time_delta[:, None, None] * velocity
    latents_ext = padded(latents_next, (("tile", 1),), 1)
    image_out = image_out.transpose(1, 0, 2).reshape(requests, tile_rows, tile_cols, model_width)
    return (image_out, text_out.transpose(1, 0, 2), latents_ext)


def solution(mesh):
    return jax.shard_map(
        per_device,
        mesh=mesh,
        in_specs=(
            P(None, "tile", "tensor", None),
            P(None, ("tile", "tensor"), None),
            P(None, "tile", "tensor"),
            P(),
            P(),
            P(),
            P(),
            P(),
            P(),
            P(),
            P(None, None, "tensor"),
            P(None, None, "tensor"),
            P("tensor", None),
            P("tensor", None),
            P(),
            P(None, "tensor"),
            P("tensor", None),
            P(),
        ),
        out_specs=(
            P(None, "tile", "tensor", None),
            P(None, ("tile", "tensor"), None),
            P(None, "tile", "tensor"),
        ),
        check_vma=False,
    )
```

```python
import math

import jax
import jax.numpy as jnp
from jax import lax
from jax.sharding import PartitionSpec as P

HEAD_DIM = 128
GRID = 32
NSTEPS = 28


norm_eps = 1e-06
time_shift = 3.0


def padded(value, sides, width):
    for axis, dim in sides:
        size, length = (lax.axis_size(axis), value.shape[dim])
        up = [(i, (i + 1) % size) for i in range(size - 1)]
        down = [(j, i) for i, j in up]
        last = lax.slice_in_dim(value, length - width, length, axis=dim)
        leading = lax.slice_in_dim(value, 0, width, axis=dim)
        before = lax.ppermute(last, axis, up)
        after = lax.ppermute(leading, axis, down)
        value = jnp.concatenate([before, value, after], axis=dim)
    return value


def layer_norm(values):
    average = jnp.mean(values, -1, keepdims=True)
    centred = values - average
    spread = jnp.mean(centred * centred, -1, keepdims=True)
    return centred * lax.rsqrt(spread + norm_eps)


def modulate(hidden, shift, stretch):
    normed = layer_norm(hidden.astype(jnp.float32))
    return ((1.0 + stretch) * normed + shift).astype(jnp.bfloat16)


def rope_tables(row_ids, col_ids):
    lane = jnp.arange(2 * 64, dtype=jnp.int32)
    pair_index = lane // 2
    row_rank = (pair_index - 8).astype(jnp.float32)
    col_rank = (pair_index - 36).astype(jnp.float32)
    log_base = math.log(10000.0)
    row_freq = jnp.where(
        (pair_index >= 8) & (pair_index < 36), jnp.exp(-2.0 * row_rank / 56.0 * log_base), 0.0
    )
    col_freq = jnp.where(pair_index >= 36, jnp.exp(-2.0 * col_rank / 56.0 * log_base), 0.0)
    angles = row_ids[..., None] * row_freq + col_ids[..., None] * col_freq
    sign_table = jnp.where(lane % 2 == 0, -1.0, 1.0).astype(jnp.float32)
    return (jnp.cos(angles), jnp.sin(angles) * sign_table)


def rotate(values, cos_table, sin_table):
    lane = lax.broadcasted_iota(jnp.int32, values.shape, values.ndim - 1)
    swapped = jnp.where(
        lane % 2 == 0, jnp.roll(values, -1, axis=-1), jnp.roll(values, 1, axis=-1)
    )
    return values * cos_table + swapped * sin_table


def head_norm(projected, head_gain):
    squares = jnp.mean(projected * projected, -1, keepdims=True)
    return projected * lax.rsqrt(squares + norm_eps) * head_gain


def sigma_of(step_float):
    level = 1.0 - step_float / NSTEPS
    return time_shift * level / (1.0 + (time_shift - 1.0) * level)


def key_usable(text_len, key_count, text_tile, block_len):
    key_pos = jnp.arange(key_count, dtype=jnp.int32)
    owner_tile = key_pos // block_len
    offset = key_pos % block_len
    text_pos = owner_tile * text_tile + offset
    return jnp.logical_or(offset[None, :] >= text_tile, text_pos[None, :] < text_len[:, None])


def sum_over_tensor(term, owners, narrow):
    if not narrow:
        return lax.psum_scatter(term, "tensor", scatter_dimension=0, tiled=True)
    parts = term.astype(jnp.bfloat16).reshape((owners, -1) + term.shape[1:])
    parts = lax.all_to_all(parts, "tensor", 0, 0, tiled=True)
    return jnp.sum(parts.astype(jnp.float32), 0)


NARROW_SUMS = True


def per_device(
    image_hidden,
    text_hidden,
    latents,
    step_index,
    anchor,
    text_len,
    mod_image,
    mod_text,
    mod_mlp,
    mod_final,
    qkv_image,
    qkv_text,
    proj_image,
    proj_text,
    qk_gain,
    mlp_expand,
    mlp_reduce,
    final_weight,
):
    requests, tile_rows, tile_cols, model_width = image_hidden.shape
    local_cols = qkv_image.shape[2]
    local_heads = local_cols // HEAD_DIM
    owners = lax.axis_size("tensor")
    own_image = tile_rows * tile_cols
    own_text = text_hidden.shape[1]
    slots = own_image + own_text
    image_own = image_hidden.reshape(requests, own_image, model_width).transpose(1, 0, 2)
    text_own = text_hidden.transpose(1, 0, 2)
    image_mod_own = modulate(image_own, mod_image[None, :, 0, :], mod_image[None, :, 1, :])
    text_mod_own = modulate(text_own, mod_text[None, :, 0, :], mod_text[None, :, 1, :])
    image_count = owners * own_image
    text_tile = owners * own_text
    block_len = text_tile + image_count
    image_mod = lax.all_gather(image_mod_own, "tensor", axis=0, tiled=True).reshape(
        image_count * requests, model_width
    )
    text_mod = lax.all_to_all(
        jnp.broadcast_to(text_mod_own[None], (owners,) + text_mod_own.shape), "tensor", 0, 0,
        tiled=True,
    ).reshape(text_tile * requests, model_width)
    tile_index = lax.axis_index("tile")
    token_index = jnp.arange(image_count, dtype=jnp.int32)
    owner = token_index // own_image
    within = token_index % own_image
    row_ids = (anchor[None, :, 0] + tile_index * tile_rows + (within // tile_cols)[:, None]).astype(
        jnp.float32
    )
    col_ids = (anchor[None, :, 1] + (owner * tile_cols + within % tile_cols)[:, None]).astype(
        jnp.float32
    )
    cos_table, sin_table = rope_tables(row_ids, col_ids)
    cos_table = cos_table[:, :, None, :]
    sin_table = sin_table[:, :, None, :]
    image_qkv = jnp.dot(
        image_mod, qkv_image.reshape(model_width, 3 * local_cols), preferred_element_type=jnp.float32
    ).reshape(image_count, requests, 3, local_heads, HEAD_DIM)
    text_qkv = jnp.dot(
        text_mod, qkv_text.reshape(model_width, 3 * local_cols), preferred_element_type=jnp.float32
    ).reshape(text_tile, requests, 3, local_heads, HEAD_DIM)
    query = jnp.concatenate(
        [
            head_norm(text_qkv[:, :, 0], qk_gain[1, 0]).astype(jnp.bfloat16),
            rotate(head_norm(image_qkv[:, :, 0], qk_gain[0, 0]), cos_table, sin_table).astype(
                jnp.bfloat16
            ),
        ],
        0,
    )
    keys = jnp.concatenate(
        [
            head_norm(text_qkv[:, :, 1], qk_gain[1, 1]).astype(jnp.bfloat16),
            rotate(head_norm(image_qkv[:, :, 1], qk_gain[0, 1]), cos_table, sin_table).astype(
                jnp.bfloat16
            ),
        ],
        0,
    )
    values = jnp.concatenate([text_qkv[:, :, 2], image_qkv[:, :, 2]], 0).astype(jnp.bfloat16)
    score_scale = 1.0 / math.sqrt(HEAD_DIM)
    kv_all = lax.all_gather(jnp.stack([keys, values], 1), "tile", axis=0, tiled=True)
    keys_all, values_all = kv_all[:, 0], kv_all[:, 1]
    usable = key_usable(text_len, keys_all.shape[0], text_tile, block_len)[:, None, None, :]
    scores = (
        jnp.einsum("qrhd,krhd->rhqk", query, keys_all, preferred_element_type=jnp.float32)
        * score_scale
    )
    row_top = jnp.max(jnp.where(usable, scores, -jnp.inf), -1, keepdims=True)
    weights_raw = jnp.where(usable, jnp.exp(scores - row_top), 0.0)
    weight_sum = jnp.sum(weights_raw, -1, keepdims=True)
    accum = jnp.einsum(
        "rhqk,krhd->rhqd",
        weights_raw.astype(jnp.bfloat16),
        values_all,
        preferred_element_type=jnp.float32,
    )
    attended = (
        (accum / weight_sum).astype(jnp.bfloat16).transpose(2, 0, 1, 3).reshape(
            block_len, requests, local_cols
        )
    )
    text_att = attended[:text_tile].reshape(text_tile * requests, local_cols)
    image_att = attended[text_tile:].reshape(image_count * requests, local_cols)
    image_term = jnp.dot(image_att, proj_image, preferred_element_type=jnp.float32).reshape(
        image_count, requests, model_width
    )
    image_sum = sum_over_tensor(image_term, owners, NARROW_SUMS)
    text_term = jnp.dot(text_att, proj_text, preferred_element_type=jnp.float32).reshape(
        text_tile, requests, model_width
    )
    after_image = (image_sum[0, 0, 0] * 0.0).astype(text_term.dtype)
    text_sum = sum_over_tensor(text_term + after_image, owners, NARROW_SUMS)
    image_mid = (image_own.astype(jnp.float32) + mod_image[None, :, 2, :] * image_sum).astype(
        jnp.bfloat16
    )
    mlp_mod = modulate(image_mid, mod_mlp[None, :, 0, :], mod_mlp[None, :, 1, :])
    piece = lax.all_gather(mlp_mod, "tensor", axis=0, tiled=True)
    grown = jnp.dot(piece.reshape(-1, model_width), mlp_expand, preferred_element_type=jnp.float32)
    activated = jax.nn.gelu(grown, approximate=True).astype(jnp.bfloat16)
    text_out = (text_own.astype(jnp.float32) + mod_text[None, :, 2, :] * text_sum).astype(
        jnp.bfloat16
    )
    mlp_term = jnp.dot(activated, mlp_reduce, preferred_element_type=jnp.float32).reshape(
        image_count, requests, model_width
    )
    mlp_sum = sum_over_tensor(mlp_term, owners, NARROW_SUMS)
    image_out = (image_mid.astype(jnp.float32) + mod_mlp[None, :, 2, :] * mlp_sum).astype(
        jnp.bfloat16
    )
    final_in = modulate(image_out, mod_final[None, :, 0, :], mod_final[None, :, 1, :])
    velocity = jnp.dot(
        final_in.reshape(own_image * requests, model_width),
        final_weight,
        preferred_element_type=jnp.float32,
    ).reshape(own_image, requests, final_weight.shape[1])
    velocity = velocity.transpose(1, 0, 2).reshape(
        requests, tile_rows, tile_cols * final_weight.shape[1]
    )
    step_float = step_index.astype(jnp.float32)
    time_delta = sigma_of(step_float + 1.0) - sigma_of(step_float)
    latents_next = latents + time_delta[:, None, None] * velocity
    latents_ext = padded(latents_next, (("tile", 1),), 1)
    image_out = image_out.transpose(1, 0, 2).reshape(requests, tile_rows, tile_cols, model_width)
    return (image_out, text_out.transpose(1, 0, 2), latents_ext)


def solution(mesh):
    return jax.shard_map(
        per_device,
        mesh=mesh,
        in_specs=(
            P(None, "tile", "tensor", None),
            P(None, ("tile", "tensor"), None),
            P(None, "tile", "tensor"),
            P(),
            P(),
            P(),
            P(),
            P(),
            P(),
            P(),
            P(None, None, "tensor"),
            P(None, None, "tensor"),
            P("tensor", None),
            P("tensor", None),
            P(),
            P(None, "tensor"),
            P("tensor", None),
            P(),
        ),
        out_specs=(
            P(None, "tile", "tensor", None),
            P(None, ("tile", "tensor"), None),
            P(None, "tile", "tensor"),
        ),
        check_vma=False,
    )
```

```python
import math

import jax
import jax.numpy as jnp
from jax import lax
from jax.sharding import PartitionSpec as P

HEAD_DIM = 128
GRID = 32
NSTEPS = 28


norm_eps = 1e-06
time_shift = 3.0


def padded(value, sides, width):
    for axis, dim in sides:
        size, length = (lax.axis_size(axis), value.shape[dim])
        up = [(i, (i + 1) % size) for i in range(size - 1)]
        down = [(j, i) for i, j in up]
        last = lax.slice_in_dim(value, length - width, length, axis=dim)
        leading = lax.slice_in_dim(value, 0, width, axis=dim)
        before = lax.ppermute(last, axis, up)
        after = lax.ppermute(leading, axis, down)
        value = jnp.concatenate([before, value, after], axis=dim)
    return value


def layer_norm(values):
    average = jnp.mean(values, -1, keepdims=True)
    centred = values - average
    spread = jnp.mean(centred * centred, -1, keepdims=True)
    return centred * lax.rsqrt(spread + norm_eps)


def modulate(hidden, shift, stretch):
    normed = layer_norm(hidden.astype(jnp.float32))
    return ((1.0 + stretch) * normed + shift).astype(jnp.bfloat16)


def rope_tables(row_ids, col_ids):
    lane = jnp.arange(2 * 64, dtype=jnp.int32)
    pair_index = lane // 2
    row_rank = (pair_index - 8).astype(jnp.float32)
    col_rank = (pair_index - 36).astype(jnp.float32)
    log_base = math.log(10000.0)
    row_freq = jnp.where(
        (pair_index >= 8) & (pair_index < 36), jnp.exp(-2.0 * row_rank / 56.0 * log_base), 0.0
    )
    col_freq = jnp.where(pair_index >= 36, jnp.exp(-2.0 * col_rank / 56.0 * log_base), 0.0)
    angles = row_ids[..., None] * row_freq + col_ids[..., None] * col_freq
    sign_table = jnp.where(lane % 2 == 0, -1.0, 1.0).astype(jnp.float32)
    return (jnp.cos(angles), jnp.sin(angles) * sign_table)


def rotate(values, cos_table, sin_table):
    lane = lax.broadcasted_iota(jnp.int32, values.shape, values.ndim - 1)
    swapped = jnp.where(
        lane % 2 == 0, jnp.roll(values, -1, axis=-1), jnp.roll(values, 1, axis=-1)
    )
    return values * cos_table + swapped * sin_table


def head_norm(projected, head_gain):
    squares = jnp.mean(projected * projected, -1, keepdims=True)
    return projected * lax.rsqrt(squares + norm_eps) * head_gain


def sigma_of(step_float):
    level = 1.0 - step_float / NSTEPS
    return time_shift * level / (1.0 + (time_shift - 1.0) * level)


def key_usable(text_len, key_count, text_tile, block_len):
    key_pos = jnp.arange(key_count, dtype=jnp.int32)
    owner_tile = key_pos // block_len
    offset = key_pos % block_len
    text_pos = owner_tile * text_tile + offset
    return jnp.logical_or(offset[None, :] >= text_tile, text_pos[None, :] < text_len[:, None])


def sum_over_tensor(term, owners, narrow):
    if not narrow:
        return lax.psum_scatter(term, "tensor", scatter_dimension=0, tiled=True)
    parts = term.astype(jnp.bfloat16).reshape((owners, -1) + term.shape[1:])
    parts = lax.all_to_all(parts, "tensor", 0, 0, tiled=True)
    return jnp.sum(parts.astype(jnp.float32), 0)


NARROW_SUMS = True


def per_device(
    image_hidden,
    text_hidden,
    latents,
    step_index,
    anchor,
    text_len,
    mod_image,
    mod_text,
    mod_mlp,
    mod_final,
    qkv_image,
    qkv_text,
    proj_image,
    proj_text,
    qk_gain,
    mlp_expand,
    mlp_reduce,
    final_weight,
):
    requests, tile_rows, tile_cols, model_width = image_hidden.shape
    local_cols = qkv_image.shape[2]
    local_heads = local_cols // HEAD_DIM
    owners = lax.axis_size("tensor")
    own_image = tile_rows * tile_cols
    own_text = text_hidden.shape[1]
    slots = own_image + own_text
    image_own = image_hidden.reshape(requests, own_image, model_width).transpose(1, 0, 2)
    text_own = text_hidden.transpose(1, 0, 2)
    image_mod_own = modulate(image_own, mod_image[None, :, 0, :], mod_image[None, :, 1, :])
    text_mod_own = modulate(text_own, mod_text[None, :, 0, :], mod_text[None, :, 1, :])
    image_count = owners * own_image
    text_tile = owners * own_text
    block_len = text_tile + image_count
    half = requests // 2
    image_sc = lax.all_gather(image_mod_own[:, :half], "tensor", axis=0, tiled=True)
    rest = jnp.concatenate(
        [
            image_mod_own[:, half:].reshape(-1, model_width),
            text_mod_own.reshape(-1, model_width),
        ],
        0,
    )
    rest = lax.all_to_all(
        jnp.broadcast_to(rest[None], (owners,) + rest.shape), "tensor", 0, 0, tiled=True
    )
    image_dma = rest[:, : own_image * (requests - half)].reshape(
        image_count, requests - half, model_width
    )
    image_mod = jnp.concatenate([image_sc, image_dma], 1).reshape(
        image_count * requests, model_width
    )
    text_mod = rest[:, own_image * (requests - half) :].reshape(text_tile * requests, model_width)
    tile_index = lax.axis_index("tile")
    token_index = jnp.arange(image_count, dtype=jnp.int32)
    owner = token_index // own_image
    within = token_index % own_image
    row_ids = (anchor[None, :, 0] + tile_index * tile_rows + (within // tile_cols)[:, None]).astype(
        jnp.float32
    )
    col_ids = (anchor[None, :, 1] + (owner * tile_cols + within % tile_cols)[:, None]).astype(
        jnp.float32
    )
    cos_table, sin_table = rope_tables(row_ids, col_ids)
    cos_table = cos_table[:, :, None, :]
    sin_table = sin_table[:, :, None, :]
    image_qkv = jnp.dot(
        image_mod, qkv_image.reshape(model_width, 3 * local_cols), preferred_element_type=jnp.float32
    ).reshape(image_count, requests, 3, local_heads, HEAD_DIM)
    text_qkv = jnp.dot(
        text_mod, qkv_text.reshape(model_width, 3 * local_cols), preferred_element_type=jnp.float32
    ).reshape(text_tile, requests, 3, local_heads, HEAD_DIM)
    query = jnp.concatenate(
        [
            head_norm(text_qkv[:, :, 0], qk_gain[1, 0]).astype(jnp.bfloat16),
            rotate(head_norm(image_qkv[:, :, 0], qk_gain[0, 0]), cos_table, sin_table).astype(
                jnp.bfloat16
            ),
        ],
        0,
    )
    keys = jnp.concatenate(
        [
            head_norm(text_qkv[:, :, 1], qk_gain[1, 1]).astype(jnp.bfloat16),
            rotate(head_norm(image_qkv[:, :, 1], qk_gain[0, 1]), cos_table, sin_table).astype(
                jnp.bfloat16
            ),
        ],
        0,
    )
    values = jnp.concatenate([text_qkv[:, :, 2], image_qkv[:, :, 2]], 0).astype(jnp.bfloat16)
    score_scale = 1.0 / math.sqrt(HEAD_DIM)
    kv_all = lax.all_gather(jnp.stack([keys, values], 1), "tile", axis=0, tiled=True)
    keys_all, values_all = kv_all[:, 0], kv_all[:, 1]
    usable = key_usable(text_len, keys_all.shape[0], text_tile, block_len)[:, None, None, :]
    scores = (
        jnp.einsum("qrhd,krhd->rhqk", query, keys_all, preferred_element_type=jnp.float32)
        * score_scale
    )
    row_top = jnp.max(jnp.where(usable, scores, -jnp.inf), -1, keepdims=True)
    weights_raw = jnp.where(usable, jnp.exp(scores - row_top), 0.0)
    weight_sum = jnp.sum(weights_raw, -1, keepdims=True)
    accum = jnp.einsum(
        "rhqk,krhd->rhqd",
        weights_raw.astype(jnp.bfloat16),
        values_all,
        preferred_element_type=jnp.float32,
    )
    attended = (
        (accum / weight_sum).astype(jnp.bfloat16).transpose(2, 0, 1, 3).reshape(
            block_len, requests, local_cols
        )
    )
    text_att = attended[:text_tile].reshape(text_tile * requests, local_cols)
    image_att = attended[text_tile:].reshape(image_count * requests, local_cols)
    image_term = jnp.dot(image_att, proj_image, preferred_element_type=jnp.float32).reshape(
        image_count, requests, model_width
    )
    image_sum = sum_over_tensor(image_term, owners, NARROW_SUMS)
    text_term = jnp.dot(text_att, proj_text, preferred_element_type=jnp.float32).reshape(
        text_tile, requests, model_width
    )
    after_image = (image_sum[0, 0, 0] * 0.0).astype(text_term.dtype)
    text_sum = sum_over_tensor(text_term + after_image, owners, NARROW_SUMS)
    image_mid = (image_own.astype(jnp.float32) + mod_image[None, :, 2, :] * image_sum).astype(
        jnp.bfloat16
    )
    mlp_mod = modulate(image_mid, mod_mlp[None, :, 0, :], mod_mlp[None, :, 1, :])
    piece = jnp.concatenate(
        [
            lax.all_gather(mlp_mod[:, :half], "tensor", axis=0, tiled=True),
            lax.all_to_all(
                jnp.broadcast_to(mlp_mod[None, :, half:], (owners,) + mlp_mod[:, half:].shape),
                "tensor",
                0,
                0,
                tiled=True,
            ).reshape(image_count, requests - half, model_width),
        ],
        1,
    )
    grown = jnp.dot(piece.reshape(-1, model_width), mlp_expand, preferred_element_type=jnp.float32)
    activated = jax.nn.gelu(grown, approximate=True).astype(jnp.bfloat16)
    text_out = (text_own.astype(jnp.float32) + mod_text[None, :, 2, :] * text_sum).astype(
        jnp.bfloat16
    )
    mlp_term = jnp.dot(activated, mlp_reduce, preferred_element_type=jnp.float32).reshape(
        image_count, requests, model_width
    )
    mlp_sum = sum_over_tensor(mlp_term, owners, NARROW_SUMS)
    image_out = (image_mid.astype(jnp.float32) + mod_mlp[None, :, 2, :] * mlp_sum).astype(
        jnp.bfloat16
    )
    final_in = modulate(image_out, mod_final[None, :, 0, :], mod_final[None, :, 1, :])
    velocity = jnp.dot(
        final_in.reshape(own_image * requests, model_width),
        final_weight,
        preferred_element_type=jnp.float32,
    ).reshape(own_image, requests, final_weight.shape[1])
    velocity = velocity.transpose(1, 0, 2).reshape(
        requests, tile_rows, tile_cols * final_weight.shape[1]
    )
    step_float = step_index.astype(jnp.float32)
    time_delta = sigma_of(step_float + 1.0) - sigma_of(step_float)
    latents_next = latents + time_delta[:, None, None] * velocity
    latents_ext = padded(latents_next, (("tile", 1),), 1)
    image_out = image_out.transpose(1, 0, 2).reshape(requests, tile_rows, tile_cols, model_width)
    return (image_out, text_out.transpose(1, 0, 2), latents_ext)


def solution(mesh):
    return jax.shard_map(
        per_device,
        mesh=mesh,
        in_specs=(
            P(None, "tile", "tensor", None),
            P(None, ("tile", "tensor"), None),
            P(None, "tile", "tensor"),
            P(),
            P(),
            P(),
            P(),
            P(),
            P(),
            P(),
            P(None, None, "tensor"),
            P(None, None, "tensor"),
            P("tensor", None),
            P("tensor", None),
            P(),
            P(None, "tensor"),
            P("tensor", None),
            P(),
        ),
        out_specs=(
            P(None, "tile", "tensor", None),
            P(None, ("tile", "tensor"), None),
            P(None, "tile", "tensor"),
        ),
        check_vma=False,
    )
```

```python
import math

import jax
import jax.numpy as jnp
from jax import lax
from jax.sharding import PartitionSpec as P

HEAD_DIM = 128
GRID = 32
NSTEPS = 28


norm_eps = 1e-06
time_shift = 3.0


def padded(value, sides, width):
    for axis, dim in sides:
        size, length = (lax.axis_size(axis), value.shape[dim])
        up = [(i, (i + 1) % size) for i in range(size - 1)]
        down = [(j, i) for i, j in up]
        last = lax.slice_in_dim(value, length - width, length, axis=dim)
        leading = lax.slice_in_dim(value, 0, width, axis=dim)
        before = lax.ppermute(last, axis, up)
        after = lax.ppermute(leading, axis, down)
        value = jnp.concatenate([before, value, after], axis=dim)
    return value


def layer_norm(values):
    average = jnp.mean(values, -1, keepdims=True)
    centred = values - average
    spread = jnp.mean(centred * centred, -1, keepdims=True)
    return centred * lax.rsqrt(spread + norm_eps)


def modulate(hidden, shift, stretch):
    normed = layer_norm(hidden.astype(jnp.float32))
    return ((1.0 + stretch) * normed + shift).astype(jnp.bfloat16)


def rope_tables(row_ids, col_ids):
    lane = jnp.arange(2 * 64, dtype=jnp.int32)
    pair_index = lane // 2
    row_rank = (pair_index - 8).astype(jnp.float32)
    col_rank = (pair_index - 36).astype(jnp.float32)
    log_base = math.log(10000.0)
    row_freq = jnp.where(
        (pair_index >= 8) & (pair_index < 36), jnp.exp(-2.0 * row_rank / 56.0 * log_base), 0.0
    )
    col_freq = jnp.where(pair_index >= 36, jnp.exp(-2.0 * col_rank / 56.0 * log_base), 0.0)
    angles = row_ids[..., None] * row_freq + col_ids[..., None] * col_freq
    sign_table = jnp.where(lane % 2 == 0, -1.0, 1.0).astype(jnp.float32)
    return (jnp.cos(angles), jnp.sin(angles) * sign_table)


def rotate(values, cos_table, sin_table):
    lane = lax.broadcasted_iota(jnp.int32, values.shape, values.ndim - 1)
    swapped = jnp.where(
        lane % 2 == 0, jnp.roll(values, -1, axis=-1), jnp.roll(values, 1, axis=-1)
    )
    return values * cos_table + swapped * sin_table


def head_norm(projected, head_gain):
    squares = jnp.mean(projected * projected, -1, keepdims=True)
    return projected * lax.rsqrt(squares + norm_eps) * head_gain


def sigma_of(step_float):
    level = 1.0 - step_float / NSTEPS
    return time_shift * level / (1.0 + (time_shift - 1.0) * level)


def key_usable(text_len, key_count, text_tile, block_len):
    key_pos = jnp.arange(key_count, dtype=jnp.int32)
    owner_tile = key_pos // block_len
    offset = key_pos % block_len
    text_pos = owner_tile * text_tile + offset
    return jnp.logical_or(offset[None, :] >= text_tile, text_pos[None, :] < text_len[:, None])


def sum_over_tensor(term, owners, narrow):
    if not narrow:
        return lax.psum_scatter(term, "tensor", scatter_dimension=0, tiled=True)
    parts = term.astype(jnp.bfloat16).reshape((owners, -1) + term.shape[1:])
    parts = lax.all_to_all(parts, "tensor", 0, 0, tiled=True)
    return jnp.sum(parts.astype(jnp.float32), 0)


NARROW_SUMS = True


def per_device(
    image_hidden,
    text_hidden,
    latents,
    step_index,
    anchor,
    text_len,
    mod_image,
    mod_text,
    mod_mlp,
    mod_final,
    qkv_image,
    qkv_text,
    proj_image,
    proj_text,
    qk_gain,
    mlp_expand,
    mlp_reduce,
    final_weight,
):
    requests, tile_rows, tile_cols, model_width = image_hidden.shape
    local_cols = qkv_image.shape[2]
    local_heads = local_cols // HEAD_DIM
    owners = lax.axis_size("tensor")
    own_image = tile_rows * tile_cols
    own_text = text_hidden.shape[1]
    slots = own_image + own_text
    image_own = image_hidden.reshape(requests, own_image, model_width).transpose(1, 0, 2)
    text_own = text_hidden.transpose(1, 0, 2)
    image_mod_own = modulate(image_own, mod_image[None, :, 0, :], mod_image[None, :, 1, :])
    text_mod_own = modulate(text_own, mod_text[None, :, 0, :], mod_text[None, :, 1, :])
    image_count = owners * own_image
    text_tile = owners * own_text
    block_len = text_tile + image_count
    image_mod = lax.all_gather(image_mod_own, "tensor", axis=0, tiled=True).reshape(
        image_count * requests, model_width
    )
    text_mod = lax.all_to_all(
        jnp.broadcast_to(text_mod_own[None], (owners,) + text_mod_own.shape), "tensor", 0, 0,
        tiled=True,
    ).reshape(text_tile * requests, model_width)
    tile_index = lax.axis_index("tile")
    token_index = jnp.arange(image_count, dtype=jnp.int32)
    owner = token_index // own_image
    within = token_index % own_image
    row_ids = (anchor[None, :, 0] + tile_index * tile_rows + (within // tile_cols)[:, None]).astype(
        jnp.float32
    )
    col_ids = (anchor[None, :, 1] + (owner * tile_cols + within % tile_cols)[:, None]).astype(
        jnp.float32
    )
    cos_table, sin_table = rope_tables(row_ids, col_ids)
    cos_table = cos_table[:, :, None, :]
    sin_table = sin_table[:, :, None, :]
    image_qkv = jnp.dot(
        image_mod, qkv_image.reshape(model_width, 3 * local_cols), preferred_element_type=jnp.float32
    ).reshape(image_count, requests, 3, local_heads, HEAD_DIM)
    text_qkv = jnp.dot(
        text_mod, qkv_text.reshape(model_width, 3 * local_cols), preferred_element_type=jnp.float32
    ).reshape(text_tile, requests, 3, local_heads, HEAD_DIM)
    query = jnp.concatenate(
        [
            head_norm(text_qkv[:, :, 0], qk_gain[1, 0]).astype(jnp.bfloat16),
            rotate(head_norm(image_qkv[:, :, 0], qk_gain[0, 0]), cos_table, sin_table).astype(
                jnp.bfloat16
            ),
        ],
        0,
    )
    keys = jnp.concatenate(
        [
            head_norm(text_qkv[:, :, 1], qk_gain[1, 1]).astype(jnp.bfloat16),
            rotate(head_norm(image_qkv[:, :, 1], qk_gain[0, 1]), cos_table, sin_table).astype(
                jnp.bfloat16
            ),
        ],
        0,
    )
    values = jnp.concatenate([text_qkv[:, :, 2], image_qkv[:, :, 2]], 0).astype(jnp.bfloat16)
    score_scale = 1.0 / math.sqrt(HEAD_DIM)
    tiles = lax.axis_size("tile")
    parts = tiles // requests
    part_len = block_len // parts
    keys_r = jnp.repeat(keys.transpose(1, 0, 2, 3), parts, axis=0)
    values_r = jnp.repeat(values.transpose(1, 0, 2, 3), parts, axis=0)
    query_r = query.transpose(1, 0, 2, 3).reshape(tiles, part_len, local_heads, HEAD_DIM)
    outgoing = jnp.concatenate([keys_r, values_r, query_r], 1)
    incoming = lax.all_to_all(outgoing, "tile", 0, 0, tiled=True)
    keys_all = incoming[:, :block_len].reshape(tiles * block_len, local_heads, HEAD_DIM)
    values_all = incoming[:, block_len : 2 * block_len].reshape(
        tiles * block_len, local_heads, HEAD_DIM
    )
    query_mine = incoming[:, 2 * block_len :].reshape(tiles * part_len, local_heads, HEAD_DIM)
    my_request = tile_index // parts
    usable = key_usable(text_len[my_request][None], keys_all.shape[0], text_tile, block_len)[
        0
    ][None, None, :]
    scores = (
        jnp.einsum("qhd,khd->hqk", query_mine, keys_all, preferred_element_type=jnp.float32)
        * score_scale
    )
    row_top = jnp.max(jnp.where(usable, scores, -jnp.inf), -1, keepdims=True)
    weights_raw = jnp.where(usable, jnp.exp(scores - row_top), 0.0)
    weight_sum = jnp.sum(weights_raw, -1, keepdims=True)
    accum = jnp.einsum(
        "hqk,khd->hqd",
        weights_raw.astype(jnp.bfloat16),
        values_all,
        preferred_element_type=jnp.float32,
    )
    attended_mine = (
        (accum / weight_sum).astype(jnp.bfloat16).transpose(1, 0, 2).reshape(
            tiles, part_len, local_heads * HEAD_DIM
        )
    )
    returned = lax.all_to_all(attended_mine, "tile", 0, 0, tiled=True)
    attended = returned.reshape(requests, block_len, local_cols).transpose(1, 0, 2)
    text_att = attended[:text_tile].reshape(text_tile * requests, local_cols)
    image_att = attended[text_tile:].reshape(image_count * requests, local_cols)
    image_term = jnp.dot(image_att, proj_image, preferred_element_type=jnp.float32).reshape(
        image_count, requests, model_width
    )
    image_sum = sum_over_tensor(image_term, owners, NARROW_SUMS)
    text_term = jnp.dot(text_att, proj_text, preferred_element_type=jnp.float32).reshape(
        text_tile, requests, model_width
    )
    after_image = (image_sum[0, 0, 0] * 0.0).astype(text_term.dtype)
    text_sum = sum_over_tensor(text_term + after_image, owners, NARROW_SUMS)
    image_mid = (image_own.astype(jnp.float32) + mod_image[None, :, 2, :] * image_sum).astype(
        jnp.bfloat16
    )
    mlp_mod = modulate(image_mid, mod_mlp[None, :, 0, :], mod_mlp[None, :, 1, :])
    piece = lax.all_gather(mlp_mod, "tensor", axis=0, tiled=True)
    grown = jnp.dot(piece.reshape(-1, model_width), mlp_expand, preferred_element_type=jnp.float32)
    activated = jax.nn.gelu(grown, approximate=True).astype(jnp.bfloat16)
    text_out = (text_own.astype(jnp.float32) + mod_text[None, :, 2, :] * text_sum).astype(
        jnp.bfloat16
    )
    mlp_term = jnp.dot(activated, mlp_reduce, preferred_element_type=jnp.float32).reshape(
        image_count, requests, model_width
    )
    mlp_sum = sum_over_tensor(mlp_term, owners, NARROW_SUMS)
    image_out = (image_mid.astype(jnp.float32) + mod_mlp[None, :, 2, :] * mlp_sum).astype(
        jnp.bfloat16
    )
    final_in = modulate(image_out, mod_final[None, :, 0, :], mod_final[None, :, 1, :])
    velocity = jnp.dot(
        final_in.reshape(own_image * requests, model_width),
        final_weight,
        preferred_element_type=jnp.float32,
    ).reshape(own_image, requests, final_weight.shape[1])
    velocity = velocity.transpose(1, 0, 2).reshape(
        requests, tile_rows, tile_cols * final_weight.shape[1]
    )
    step_float = step_index.astype(jnp.float32)
    time_delta = sigma_of(step_float + 1.0) - sigma_of(step_float)
    latents_next = latents + time_delta[:, None, None] * velocity
    latents_ext = padded(latents_next, (("tile", 1),), 1)
    image_out = image_out.transpose(1, 0, 2).reshape(requests, tile_rows, tile_cols, model_width)
    return (image_out, text_out.transpose(1, 0, 2), latents_ext)


def solution(mesh):
    return jax.shard_map(
        per_device,
        mesh=mesh,
        in_specs=(
            P(None, "tile", "tensor", None),
            P(None, ("tile", "tensor"), None),
            P(None, "tile", "tensor"),
            P(),
            P(),
            P(),
            P(),
            P(),
            P(),
            P(),
            P(None, None, "tensor"),
            P(None, None, "tensor"),
            P("tensor", None),
            P("tensor", None),
            P(),
            P(None, "tensor"),
            P("tensor", None),
            P(),
        ),
        out_specs=(
            P(None, "tile", "tensor", None),
            P(None, ("tile", "tensor"), None),
            P(None, "tile", "tensor"),
        ),
        check_vma=False,
    )
```

```python
import math

import jax
import jax.numpy as jnp
from jax import lax
from jax.sharding import PartitionSpec as P

HEAD_DIM = 128
GRID = 32
NSTEPS = 28


norm_eps = 1e-06
time_shift = 3.0


def padded(value, sides, width):
    for axis, dim in sides:
        size, length = (lax.axis_size(axis), value.shape[dim])
        up = [(i, (i + 1) % size) for i in range(size - 1)]
        down = [(j, i) for i, j in up]
        last = lax.slice_in_dim(value, length - width, length, axis=dim)
        leading = lax.slice_in_dim(value, 0, width, axis=dim)
        before = lax.ppermute(last, axis, up)
        after = lax.ppermute(leading, axis, down)
        value = jnp.concatenate([before, value, after], axis=dim)
    return value


def layer_norm(values):
    average = jnp.mean(values, -1, keepdims=True)
    centred = values - average
    spread = jnp.mean(centred * centred, -1, keepdims=True)
    return centred * lax.rsqrt(spread + norm_eps)


def modulate(hidden, shift, stretch):
    normed = layer_norm(hidden.astype(jnp.float32))
    return ((1.0 + stretch) * normed + shift).astype(jnp.bfloat16)


def rope_tables(row_ids, col_ids):
    lane = jnp.arange(2 * 64, dtype=jnp.int32)
    pair_index = lane // 2
    row_rank = (pair_index - 8).astype(jnp.float32)
    col_rank = (pair_index - 36).astype(jnp.float32)
    log_base = math.log(10000.0)
    row_freq = jnp.where(
        (pair_index >= 8) & (pair_index < 36), jnp.exp(-2.0 * row_rank / 56.0 * log_base), 0.0
    )
    col_freq = jnp.where(pair_index >= 36, jnp.exp(-2.0 * col_rank / 56.0 * log_base), 0.0)
    angles = row_ids[..., None] * row_freq + col_ids[..., None] * col_freq
    sign_table = jnp.where(lane % 2 == 0, -1.0, 1.0).astype(jnp.float32)
    return (jnp.cos(angles), jnp.sin(angles) * sign_table)


def rotate(values, cos_table, sin_table):
    lane = lax.broadcasted_iota(jnp.int32, values.shape, values.ndim - 1)
    swapped = jnp.where(
        lane % 2 == 0, jnp.roll(values, -1, axis=-1), jnp.roll(values, 1, axis=-1)
    )
    return values * cos_table + swapped * sin_table


def head_norm(projected, head_gain):
    squares = jnp.mean(projected * projected, -1, keepdims=True)
    return projected * lax.rsqrt(squares + norm_eps) * head_gain


def sigma_of(step_float):
    level = 1.0 - step_float / NSTEPS
    return time_shift * level / (1.0 + (time_shift - 1.0) * level)


def key_usable(text_len, key_count, text_tile, block_len):
    key_pos = jnp.arange(key_count, dtype=jnp.int32)
    owner_tile = key_pos // block_len
    offset = key_pos % block_len
    text_pos = owner_tile * text_tile + offset
    return jnp.logical_or(offset[None, :] >= text_tile, text_pos[None, :] < text_len[:, None])


def sum_over_tensor(term, owners, narrow):
    if not narrow:
        return lax.psum_scatter(term, "tensor", scatter_dimension=0, tiled=True)
    parts = term.astype(jnp.bfloat16).reshape((owners, -1) + term.shape[1:])
    parts = lax.all_to_all(parts, "tensor", 0, 0, tiled=True)
    return jnp.sum(parts.astype(jnp.float32), 0)


NARROW_SUMS = True


def per_device(
    image_hidden,
    text_hidden,
    latents,
    step_index,
    anchor,
    text_len,
    mod_image,
    mod_text,
    mod_mlp,
    mod_final,
    qkv_image,
    qkv_text,
    proj_image,
    proj_text,
    qk_gain,
    mlp_expand,
    mlp_reduce,
    final_weight,
):
    requests, tile_rows, tile_cols, model_width = image_hidden.shape
    local_cols = qkv_image.shape[2]
    local_heads = local_cols // HEAD_DIM
    owners = lax.axis_size("tensor")
    own_image = tile_rows * tile_cols
    own_text = text_hidden.shape[1]
    slots = own_image + own_text
    image_own = image_hidden.reshape(requests, own_image, model_width).transpose(1, 0, 2)
    text_own = text_hidden.transpose(1, 0, 2)
    image_mod_own = modulate(image_own, mod_image[None, :, 0, :], mod_image[None, :, 1, :])
    text_mod_own = modulate(text_own, mod_text[None, :, 0, :], mod_text[None, :, 1, :])
    image_count = owners * own_image
    text_tile = owners * own_text
    block_len = text_tile + image_count
    joined = jnp.concatenate([image_mod_own, text_mod_own], 0)
    gathered = lax.all_to_all(
        jnp.broadcast_to(joined[None], (owners,) + joined.shape), "tensor", 0, 0, tiled=True
    )
    image_mod = gathered[:, :own_image].reshape(image_count * requests, model_width)
    text_mod = gathered[:, own_image:].reshape(text_tile * requests, model_width)
    tile_index = lax.axis_index("tile")
    token_index = jnp.arange(image_count, dtype=jnp.int32)
    owner = token_index // own_image
    within = token_index % own_image
    row_ids = (anchor[None, :, 0] + tile_index * tile_rows + (within // tile_cols)[:, None]).astype(
        jnp.float32
    )
    col_ids = (anchor[None, :, 1] + (owner * tile_cols + within % tile_cols)[:, None]).astype(
        jnp.float32
    )
    cos_table, sin_table = rope_tables(row_ids, col_ids)
    cos_table = cos_table[:, :, None, :]
    sin_table = sin_table[:, :, None, :]
    image_qkv = jnp.dot(
        image_mod, qkv_image.reshape(model_width, 3 * local_cols), preferred_element_type=jnp.float32
    ).reshape(image_count, requests, 3, local_heads, HEAD_DIM)
    text_qkv = jnp.dot(
        text_mod, qkv_text.reshape(model_width, 3 * local_cols), preferred_element_type=jnp.float32
    ).reshape(text_tile, requests, 3, local_heads, HEAD_DIM)
    query = jnp.concatenate(
        [
            head_norm(text_qkv[:, :, 0], qk_gain[1, 0]).astype(jnp.bfloat16),
            rotate(head_norm(image_qkv[:, :, 0], qk_gain[0, 0]), cos_table, sin_table).astype(
                jnp.bfloat16
            ),
        ],
        0,
    )
    keys = jnp.concatenate(
        [
            head_norm(text_qkv[:, :, 1], qk_gain[1, 1]).astype(jnp.bfloat16),
            rotate(head_norm(image_qkv[:, :, 1], qk_gain[0, 1]), cos_table, sin_table).astype(
                jnp.bfloat16
            ),
        ],
        0,
    )
    values = jnp.concatenate([text_qkv[:, :, 2], image_qkv[:, :, 2]], 0).astype(jnp.bfloat16)
    score_scale = 1.0 / math.sqrt(HEAD_DIM)
    tiles = lax.axis_size("tile")
    parts = tiles // requests
    part_len = block_len // parts
    keys_r = jnp.repeat(keys.transpose(1, 0, 2, 3), parts, axis=0)
    values_r = jnp.repeat(values.transpose(1, 0, 2, 3), parts, axis=0)
    query_r = query.transpose(1, 0, 2, 3).reshape(tiles, part_len, local_heads, HEAD_DIM)
    outgoing = jnp.concatenate([keys_r, values_r, query_r], 1)
    incoming = lax.all_to_all(outgoing, "tile", 0, 0, tiled=True)
    keys_all = incoming[:, :block_len].reshape(tiles * block_len, local_heads, HEAD_DIM)
    values_all = incoming[:, block_len : 2 * block_len].reshape(
        tiles * block_len, local_heads, HEAD_DIM
    )
    query_mine = incoming[:, 2 * block_len :].reshape(tiles * part_len, local_heads, HEAD_DIM)
    my_request = tile_index // parts
    usable = key_usable(text_len[my_request][None], keys_all.shape[0], text_tile, block_len)[
        0
    ][None, None, :]
    scores = (
        jnp.einsum("qhd,khd->hqk", query_mine, keys_all, preferred_element_type=jnp.float32)
        * score_scale
    )
    row_top = jnp.max(jnp.where(usable, scores, -jnp.inf), -1, keepdims=True)
    weights_raw = jnp.where(usable, jnp.exp(scores - row_top), 0.0)
    weight_sum = jnp.sum(weights_raw, -1, keepdims=True)
    accum = jnp.einsum(
        "hqk,khd->hqd",
        weights_raw.astype(jnp.bfloat16),
        values_all,
        preferred_element_type=jnp.float32,
    )
    attended_mine = (
        (accum / weight_sum).astype(jnp.bfloat16).transpose(1, 0, 2).reshape(
            tiles, part_len, local_heads * HEAD_DIM
        )
    )
    returned = lax.all_to_all(attended_mine, "tile", 0, 0, tiled=True)
    attended = returned.reshape(requests, block_len, local_cols).transpose(1, 0, 2)
    text_att = attended[:text_tile].reshape(text_tile * requests, local_cols)
    image_att = attended[text_tile:].reshape(image_count * requests, local_cols)
    image_term = jnp.dot(image_att, proj_image, preferred_element_type=jnp.float32).reshape(
        image_count, requests, model_width
    )
    image_sum = sum_over_tensor(image_term, owners, NARROW_SUMS)
    text_term = jnp.dot(text_att, proj_text, preferred_element_type=jnp.float32).reshape(
        text_tile, requests, model_width
    )
    after_image = (image_sum[0, 0, 0] * 0.0).astype(text_term.dtype)
    text_sum = sum_over_tensor(text_term + after_image, owners, NARROW_SUMS)
    image_mid = (image_own.astype(jnp.float32) + mod_image[None, :, 2, :] * image_sum).astype(
        jnp.bfloat16
    )
    mlp_mod = modulate(image_mid, mod_mlp[None, :, 0, :], mod_mlp[None, :, 1, :])
    piece = lax.all_to_all(
        jnp.broadcast_to(mlp_mod[None], (owners,) + mlp_mod.shape), "tensor", 0, 0, tiled=True
    ).reshape(image_count, requests, model_width)
    grown = jnp.dot(piece.reshape(-1, model_width), mlp_expand, preferred_element_type=jnp.float32)
    activated = jax.nn.gelu(grown, approximate=True).astype(jnp.bfloat16)
    text_out = (text_own.astype(jnp.float32) + mod_text[None, :, 2, :] * text_sum).astype(
        jnp.bfloat16
    )
    mlp_term = jnp.dot(activated, mlp_reduce, preferred_element_type=jnp.float32).reshape(
        image_count, requests, model_width
    )
    mlp_sum = sum_over_tensor(mlp_term, owners, NARROW_SUMS)
    image_out = (image_mid.astype(jnp.float32) + mod_mlp[None, :, 2, :] * mlp_sum).astype(
        jnp.bfloat16
    )
    final_in = modulate(image_out, mod_final[None, :, 0, :], mod_final[None, :, 1, :])
    velocity = jnp.dot(
        final_in.reshape(own_image * requests, model_width),
        final_weight,
        preferred_element_type=jnp.float32,
    ).reshape(own_image, requests, final_weight.shape[1])
    velocity = velocity.transpose(1, 0, 2).reshape(
        requests, tile_rows, tile_cols * final_weight.shape[1]
    )
    step_float = step_index.astype(jnp.float32)
    time_delta = sigma_of(step_float + 1.0) - sigma_of(step_float)
    latents_next = latents + time_delta[:, None, None] * velocity
    latents_ext = padded(latents_next, (("tile", 1),), 1)
    image_out = image_out.transpose(1, 0, 2).reshape(requests, tile_rows, tile_cols, model_width)
    return (image_out, text_out.transpose(1, 0, 2), latents_ext)


def solution(mesh):
    return jax.shard_map(
        per_device,
        mesh=mesh,
        in_specs=(
            P(None, "tile", "tensor", None),
            P(None, ("tile", "tensor"), None),
            P(None, "tile", "tensor"),
            P(),
            P(),
            P(),
            P(),
            P(),
            P(),
            P(),
            P(None, None, "tensor"),
            P(None, None, "tensor"),
            P("tensor", None),
            P("tensor", None),
            P(),
            P(None, "tensor"),
            P("tensor", None),
            P(),
        ),
        out_specs=(
            P(None, "tile", "tensor", None),
            P(None, ("tile", "tensor"), None),
            P(None, "tile", "tensor"),
        ),
        check_vma=False,
    )
```

```python
import math

import jax
import jax.numpy as jnp
from jax import lax
from jax.sharding import PartitionSpec as P

HEAD_DIM = 128
GRID = 32
NSTEPS = 28


norm_eps = 1e-06
time_shift = 3.0


def padded(value, sides, width):
    for axis, dim in sides:
        size, length = (lax.axis_size(axis), value.shape[dim])
        up = [(i, (i + 1) % size) for i in range(size - 1)]
        down = [(j, i) for i, j in up]
        last = lax.slice_in_dim(value, length - width, length, axis=dim)
        leading = lax.slice_in_dim(value, 0, width, axis=dim)
        before = lax.ppermute(last, axis, up)
        after = lax.ppermute(leading, axis, down)
        value = jnp.concatenate([before, value, after], axis=dim)
    return value


def layer_norm(values):
    average = jnp.mean(values, -1, keepdims=True)
    centred = values - average
    spread = jnp.mean(centred * centred, -1, keepdims=True)
    return centred * lax.rsqrt(spread + norm_eps)


def modulate(hidden, shift, stretch):
    normed = layer_norm(hidden.astype(jnp.float32))
    return ((1.0 + stretch) * normed + shift).astype(jnp.bfloat16)


def rope_tables(row_ids, col_ids):
    lane = jnp.arange(2 * 64, dtype=jnp.int32)
    pair_index = lane // 2
    row_rank = (pair_index - 8).astype(jnp.float32)
    col_rank = (pair_index - 36).astype(jnp.float32)
    log_base = math.log(10000.0)
    row_freq = jnp.where(
        (pair_index >= 8) & (pair_index < 36), jnp.exp(-2.0 * row_rank / 56.0 * log_base), 0.0
    )
    col_freq = jnp.where(pair_index >= 36, jnp.exp(-2.0 * col_rank / 56.0 * log_base), 0.0)
    angles = row_ids[..., None] * row_freq + col_ids[..., None] * col_freq
    sign_table = jnp.where(lane % 2 == 0, -1.0, 1.0).astype(jnp.float32)
    return (jnp.cos(angles), jnp.sin(angles) * sign_table)


def rotate(values, cos_table, sin_table):
    lane = lax.broadcasted_iota(jnp.int32, values.shape, values.ndim - 1)
    swapped = jnp.where(
        lane % 2 == 0, jnp.roll(values, -1, axis=-1), jnp.roll(values, 1, axis=-1)
    )
    return values * cos_table + swapped * sin_table


def head_norm(projected, head_gain):
    squares = jnp.mean(projected * projected, -1, keepdims=True)
    return projected * lax.rsqrt(squares + norm_eps) * head_gain


def sigma_of(step_float):
    level = 1.0 - step_float / NSTEPS
    return time_shift * level / (1.0 + (time_shift - 1.0) * level)


def key_usable(text_len, key_count, text_tile, block_len):
    key_pos = jnp.arange(key_count, dtype=jnp.int32)
    owner_tile = key_pos // block_len
    offset = key_pos % block_len
    text_pos = owner_tile * text_tile + offset
    return jnp.logical_or(offset[None, :] >= text_tile, text_pos[None, :] < text_len[:, None])


def sum_over_tensor(term, owners, narrow):
    if not narrow:
        return lax.psum_scatter(term, "tensor", scatter_dimension=0, tiled=True)
    parts = term.astype(jnp.bfloat16).reshape((owners, -1) + term.shape[1:])
    parts = lax.all_to_all(parts, "tensor", 0, 0, tiled=True)
    return jnp.sum(parts.astype(jnp.float32), 0)


NARROW_SUMS = True


def per_device(
    image_hidden,
    text_hidden,
    latents,
    step_index,
    anchor,
    text_len,
    mod_image,
    mod_text,
    mod_mlp,
    mod_final,
    qkv_image,
    qkv_text,
    proj_image,
    proj_text,
    qk_gain,
    mlp_expand,
    mlp_reduce,
    final_weight,
):
    requests, tile_rows, tile_cols, model_width = image_hidden.shape
    local_cols = qkv_image.shape[2]
    local_heads = local_cols // HEAD_DIM
    owners = lax.axis_size("tensor")
    own_image = tile_rows * tile_cols
    own_text = text_hidden.shape[1]
    slots = own_image + own_text
    image_own = image_hidden.reshape(requests, own_image, model_width).transpose(1, 0, 2)
    text_own = text_hidden.transpose(1, 0, 2)
    image_mod_own = modulate(image_own, mod_image[None, :, 0, :], mod_image[None, :, 1, :])
    text_mod_own = modulate(text_own, mod_text[None, :, 0, :], mod_text[None, :, 1, :])
    image_count = owners * own_image
    text_tile = owners * own_text
    block_len = text_tile + image_count
    image_mod = lax.all_gather(image_mod_own, "tensor", axis=0, tiled=True).reshape(
        image_count * requests, model_width
    )
    text_mod = lax.all_to_all(
        jnp.broadcast_to(text_mod_own[None], (owners,) + text_mod_own.shape), "tensor", 0, 0,
        tiled=True,
    ).reshape(text_tile * requests, model_width)
    tile_index = lax.axis_index("tile")
    token_index = jnp.arange(image_count, dtype=jnp.int32)
    owner = token_index // own_image
    within = token_index % own_image
    row_ids = (anchor[None, :, 0] + tile_index * tile_rows + (within // tile_cols)[:, None]).astype(
        jnp.float32
    )
    col_ids = (anchor[None, :, 1] + (owner * tile_cols + within % tile_cols)[:, None]).astype(
        jnp.float32
    )
    cos_table, sin_table = rope_tables(row_ids, col_ids)
    cos_table = cos_table[:, :, None, :]
    sin_table = sin_table[:, :, None, :]
    image_qkv = jnp.dot(
        image_mod, qkv_image.reshape(model_width, 3 * local_cols), preferred_element_type=jnp.float32
    ).reshape(image_count, requests, 3, local_heads, HEAD_DIM)
    text_qkv = jnp.dot(
        text_mod, qkv_text.reshape(model_width, 3 * local_cols), preferred_element_type=jnp.float32
    ).reshape(text_tile, requests, 3, local_heads, HEAD_DIM)
    query = jnp.concatenate(
        [
            head_norm(text_qkv[:, :, 0], qk_gain[1, 0]).astype(jnp.bfloat16),
            rotate(head_norm(image_qkv[:, :, 0], qk_gain[0, 0]), cos_table, sin_table).astype(
                jnp.bfloat16
            ),
        ],
        0,
    )
    keys = jnp.concatenate(
        [
            head_norm(text_qkv[:, :, 1], qk_gain[1, 1]).astype(jnp.bfloat16),
            rotate(head_norm(image_qkv[:, :, 1], qk_gain[0, 1]), cos_table, sin_table).astype(
                jnp.bfloat16
            ),
        ],
        0,
    )
    values = jnp.concatenate([text_qkv[:, :, 2], image_qkv[:, :, 2]], 0).astype(jnp.bfloat16)
    score_scale = 1.0 / math.sqrt(HEAD_DIM)
    tiles = lax.axis_size("tile")
    parts = tiles // requests
    part_len = block_len // parts
    keys_r = jnp.repeat(keys.transpose(1, 0, 2, 3), parts, axis=0)
    values_r = jnp.repeat(values.transpose(1, 0, 2, 3), parts, axis=0)
    query_r = query.transpose(1, 0, 2, 3).reshape(tiles, part_len, local_heads, HEAD_DIM)
    outgoing = jnp.concatenate([keys_r, values_r, query_r], 1)
    incoming = lax.all_to_all(outgoing, "tile", 0, 0, tiled=True)
    keys_all = incoming[:, :block_len].reshape(tiles * block_len, local_heads, HEAD_DIM)
    values_all = incoming[:, block_len : 2 * block_len].reshape(
        tiles * block_len, local_heads, HEAD_DIM
    )
    query_mine = incoming[:, 2 * block_len :].reshape(tiles * part_len, local_heads, HEAD_DIM)
    my_request = tile_index // parts
    usable = key_usable(text_len[my_request][None], keys_all.shape[0], text_tile, block_len)[
        0
    ][None, None, :]
    scores = (
        jnp.einsum("qhd,khd->hqk", query_mine, keys_all, preferred_element_type=jnp.float32)
        * score_scale
    )
    row_top = jnp.max(jnp.where(usable, scores, -jnp.inf), -1, keepdims=True)
    weights_raw = jnp.where(usable, jnp.exp(scores - row_top), 0.0)
    weight_sum = jnp.sum(weights_raw, -1, keepdims=True)
    accum = jnp.einsum(
        "hqk,khd->hqd",
        weights_raw.astype(jnp.bfloat16),
        values_all,
        preferred_element_type=jnp.float32,
    )
    attended_mine = (
        (accum / weight_sum).astype(jnp.bfloat16).transpose(1, 0, 2).reshape(
            tiles, part_len, local_heads * HEAD_DIM
        )
    )
    returned = lax.all_to_all(attended_mine, "tile", 0, 0, tiled=True)
    attended = returned.reshape(requests, block_len, local_cols).transpose(1, 0, 2)
    text_att = attended[:text_tile].reshape(text_tile * requests, local_cols)
    image_att = attended[text_tile:].reshape(image_count * requests, local_cols)
    image_term = jnp.dot(image_att, proj_image, preferred_element_type=jnp.float32).reshape(
        image_count, requests, model_width
    )
    image_sum = sum_over_tensor(image_term, owners, NARROW_SUMS)
    text_term = jnp.dot(text_att, proj_text, preferred_element_type=jnp.float32).reshape(
        text_tile, requests, model_width
    )
    after_image = (image_sum[0, 0, 0] * 0.0).astype(text_term.dtype)
    text_sum = sum_over_tensor(text_term + after_image, owners, NARROW_SUMS)
    image_mid = (image_own.astype(jnp.float32) + mod_image[None, :, 2, :] * image_sum).astype(
        jnp.bfloat16
    )
    mlp_mod = modulate(image_mid, mod_mlp[None, :, 0, :], mod_mlp[None, :, 1, :])
    piece = lax.all_gather(mlp_mod, "tensor", axis=0, tiled=True)
    text_out = (text_own.astype(jnp.float32) + mod_text[None, :, 2, :] * text_sum).astype(
        jnp.bfloat16
    )
    half = requests // 2
    image_outs, velocities = [], []
    for lo, hi in ((0, half), (half, requests)):
        grown = jnp.dot(
            piece[:, lo:hi].reshape(-1, model_width), mlp_expand, preferred_element_type=jnp.float32
        )
        activated = jax.nn.gelu(grown, approximate=True).astype(jnp.bfloat16)
        mlp_term = jnp.dot(activated, mlp_reduce, preferred_element_type=jnp.float32).reshape(
            image_count, hi - lo, model_width
        )
        mlp_sum = sum_over_tensor(mlp_term, owners, NARROW_SUMS)
        image_out = (
            image_mid[:, lo:hi].astype(jnp.float32) + mod_mlp[None, lo:hi, 2, :] * mlp_sum
        ).astype(jnp.bfloat16)
        final_in = modulate(image_out, mod_final[None, lo:hi, 0, :], mod_final[None, lo:hi, 1, :])
        velocity = jnp.dot(
            final_in.reshape(own_image * (hi - lo), model_width),
            final_weight,
            preferred_element_type=jnp.float32,
        ).reshape(own_image, hi - lo, final_weight.shape[1])
        image_outs.append(image_out)
        velocities.append(velocity)
    image_out = jnp.concatenate(image_outs, 1)
    velocity = jnp.concatenate(velocities, 1).transpose(1, 0, 2).reshape(
        requests, tile_rows, tile_cols * final_weight.shape[1]
    )
    step_float = step_index.astype(jnp.float32)
    time_delta = sigma_of(step_float + 1.0) - sigma_of(step_float)
    latents_next = latents + time_delta[:, None, None] * velocity
    latents_ext = padded(latents_next, (("tile", 1),), 1)
    image_out = image_out.transpose(1, 0, 2).reshape(requests, tile_rows, tile_cols, model_width)
    return (image_out, text_out.transpose(1, 0, 2), latents_ext)


def solution(mesh):
    return jax.shard_map(
        per_device,
        mesh=mesh,
        in_specs=(
            P(None, "tile", "tensor", None),
            P(None, ("tile", "tensor"), None),
            P(None, "tile", "tensor"),
            P(),
            P(),
            P(),
            P(),
            P(),
            P(),
            P(),
            P(None, None, "tensor"),
            P(None, None, "tensor"),
            P("tensor", None),
            P("tensor", None),
            P(),
            P(None, "tensor"),
            P("tensor", None),
            P(),
        ),
        out_specs=(
            P(None, "tile", "tensor", None),
            P(None, ("tile", "tensor"), None),
            P(None, "tile", "tensor"),
        ),
        check_vma=False,
    )
```

```python
import math

import jax
import jax.numpy as jnp
from jax import lax
from jax.sharding import PartitionSpec as P

HEAD_DIM = 128
GRID = 32
NSTEPS = 28


norm_eps = 1e-06
time_shift = 3.0


def padded(value, sides, width):
    for axis, dim in sides:
        size, length = (lax.axis_size(axis), value.shape[dim])
        up = [(i, (i + 1) % size) for i in range(size - 1)]
        down = [(j, i) for i, j in up]
        last = lax.slice_in_dim(value, length - width, length, axis=dim)
        leading = lax.slice_in_dim(value, 0, width, axis=dim)
        before = lax.ppermute(last, axis, up)
        after = lax.ppermute(leading, axis, down)
        value = jnp.concatenate([before, value, after], axis=dim)
    return value


def layer_norm(values):
    average = jnp.mean(values, -1, keepdims=True)
    centred = values - average
    spread = jnp.mean(centred * centred, -1, keepdims=True)
    return centred * lax.rsqrt(spread + norm_eps)


def modulate(hidden, shift, stretch):
    normed = layer_norm(hidden.astype(jnp.float32))
    return ((1.0 + stretch) * normed + shift).astype(jnp.bfloat16)


def rope_tables(row_ids, col_ids):
    lane = jnp.arange(2 * 64, dtype=jnp.int32)
    pair_index = lane // 2
    row_rank = (pair_index - 8).astype(jnp.float32)
    col_rank = (pair_index - 36).astype(jnp.float32)
    log_base = math.log(10000.0)
    row_freq = jnp.where(
        (pair_index >= 8) & (pair_index < 36), jnp.exp(-2.0 * row_rank / 56.0 * log_base), 0.0
    )
    col_freq = jnp.where(pair_index >= 36, jnp.exp(-2.0 * col_rank / 56.0 * log_base), 0.0)
    angles = row_ids[..., None] * row_freq + col_ids[..., None] * col_freq
    sign_table = jnp.where(lane % 2 == 0, -1.0, 1.0).astype(jnp.float32)
    return (jnp.cos(angles), jnp.sin(angles) * sign_table)


def rotate(values, cos_table, sin_table):
    lane = lax.broadcasted_iota(jnp.int32, values.shape, values.ndim - 1)
    swapped = jnp.where(
        lane % 2 == 0, jnp.roll(values, -1, axis=-1), jnp.roll(values, 1, axis=-1)
    )
    return values * cos_table + swapped * sin_table


def head_norm(projected, head_gain):
    squares = jnp.mean(projected * projected, -1, keepdims=True)
    return projected * lax.rsqrt(squares + norm_eps) * head_gain


def sigma_of(step_float):
    level = 1.0 - step_float / NSTEPS
    return time_shift * level / (1.0 + (time_shift - 1.0) * level)


def key_usable(text_len, key_count, text_tile, block_len):
    key_pos = jnp.arange(key_count, dtype=jnp.int32)
    owner_tile = key_pos // block_len
    offset = key_pos % block_len
    text_pos = owner_tile * text_tile + offset
    return jnp.logical_or(offset[None, :] >= text_tile, text_pos[None, :] < text_len[:, None])


def sum_over_tensor(term, owners, narrow):
    if not narrow:
        return lax.psum_scatter(term, "tensor", scatter_dimension=0, tiled=True)
    parts = term.astype(jnp.bfloat16).reshape((owners, -1) + term.shape[1:])
    parts = lax.all_to_all(parts, "tensor", 0, 0, tiled=True)
    return jnp.sum(parts.astype(jnp.float32), 0)


NARROW_SUMS = True


def per_device(
    image_hidden,
    text_hidden,
    latents,
    step_index,
    anchor,
    text_len,
    mod_image,
    mod_text,
    mod_mlp,
    mod_final,
    qkv_image,
    qkv_text,
    proj_image,
    proj_text,
    qk_gain,
    mlp_expand,
    mlp_reduce,
    final_weight,
):
    requests, tile_rows, tile_cols, model_width = image_hidden.shape
    local_cols = qkv_image.shape[2]
    local_heads = local_cols // HEAD_DIM
    owners = lax.axis_size("tensor")
    own_image = tile_rows * tile_cols
    own_text = text_hidden.shape[1]
    slots = own_image + own_text
    image_own = image_hidden.reshape(requests, own_image, model_width).transpose(1, 0, 2)
    text_own = text_hidden.transpose(1, 0, 2)
    image_mod_own = modulate(image_own, mod_image[None, :, 0, :], mod_image[None, :, 1, :])
    text_mod_own = modulate(text_own, mod_text[None, :, 0, :], mod_text[None, :, 1, :])
    image_count = owners * own_image
    text_tile = owners * own_text
    block_len = text_tile + image_count
    joined = jnp.concatenate([image_mod_own, text_mod_own], 0)
    gathered = lax.all_gather(joined, "tensor", axis=0, tiled=True).reshape(
        owners, slots, requests, model_width
    )
    image_mod = gathered[:, :own_image].reshape(image_count * requests, model_width)
    text_mod = gathered[:, own_image:].reshape(text_tile * requests, model_width)
    tile_index = lax.axis_index("tile")
    token_index = jnp.arange(image_count, dtype=jnp.int32)
    owner = token_index // own_image
    within = token_index % own_image
    row_ids = (anchor[None, :, 0] + tile_index * tile_rows + (within // tile_cols)[:, None]).astype(
        jnp.float32
    )
    col_ids = (anchor[None, :, 1] + (owner * tile_cols + within % tile_cols)[:, None]).astype(
        jnp.float32
    )
    cos_table, sin_table = rope_tables(row_ids, col_ids)
    cos_table = cos_table[:, :, None, :]
    sin_table = sin_table[:, :, None, :]
    image_qkv = jnp.dot(
        image_mod, qkv_image.reshape(model_width, 3 * local_cols), preferred_element_type=jnp.float32
    ).reshape(image_count, requests, 3, local_heads, HEAD_DIM)
    text_qkv = jnp.dot(
        text_mod, qkv_text.reshape(model_width, 3 * local_cols), preferred_element_type=jnp.float32
    ).reshape(text_tile, requests, 3, local_heads, HEAD_DIM)
    query = jnp.concatenate(
        [
            head_norm(text_qkv[:, :, 0], qk_gain[1, 0]).astype(jnp.bfloat16),
            rotate(head_norm(image_qkv[:, :, 0], qk_gain[0, 0]), cos_table, sin_table).astype(
                jnp.bfloat16
            ),
        ],
        0,
    )
    keys = jnp.concatenate(
        [
            head_norm(text_qkv[:, :, 1], qk_gain[1, 1]).astype(jnp.bfloat16),
            rotate(head_norm(image_qkv[:, :, 1], qk_gain[0, 1]), cos_table, sin_table).astype(
                jnp.bfloat16
            ),
        ],
        0,
    )
    values = jnp.concatenate([text_qkv[:, :, 2], image_qkv[:, :, 2]], 0).astype(jnp.bfloat16)
    score_scale = 1.0 / math.sqrt(HEAD_DIM)
    tiles = lax.axis_size("tile")
    parts = tiles // requests
    part_len = block_len // parts
    keys_r = jnp.repeat(keys.transpose(1, 0, 2, 3), parts, axis=0)
    values_r = jnp.repeat(values.transpose(1, 0, 2, 3), parts, axis=0)
    query_r = query.transpose(1, 0, 2, 3).reshape(tiles, part_len, local_heads, HEAD_DIM)
    outgoing = jnp.concatenate([keys_r, values_r, query_r], 1)
    incoming = lax.all_to_all(outgoing, "tile", 0, 0, tiled=True)
    keys_all = incoming[:, :block_len].reshape(tiles * block_len, local_heads, HEAD_DIM)
    values_all = incoming[:, block_len : 2 * block_len].reshape(
        tiles * block_len, local_heads, HEAD_DIM
    )
    query_mine = incoming[:, 2 * block_len :].reshape(tiles * part_len, local_heads, HEAD_DIM)
    my_request = tile_index // parts
    usable = key_usable(text_len[my_request][None], keys_all.shape[0], text_tile, block_len)[
        0
    ][None, None, :]
    scores = (
        jnp.einsum("qhd,khd->hqk", query_mine, keys_all, preferred_element_type=jnp.float32)
        * score_scale
    )
    row_top = jnp.max(jnp.where(usable, scores, -jnp.inf), -1, keepdims=True)
    weights_raw = jnp.where(usable, jnp.exp(scores - row_top), 0.0)
    weight_sum = jnp.sum(weights_raw, -1, keepdims=True)
    accum = jnp.einsum(
        "hqk,khd->hqd",
        weights_raw.astype(jnp.bfloat16),
        values_all,
        preferred_element_type=jnp.float32,
    )
    attended_mine = (
        (accum / weight_sum).astype(jnp.bfloat16).transpose(1, 0, 2).reshape(
            tiles, part_len, local_heads * HEAD_DIM
        )
    )
    returned = lax.all_to_all(attended_mine, "tile", 0, 0, tiled=True)
    attended = returned.reshape(requests, block_len, local_cols).transpose(1, 0, 2)
    text_att = attended[:text_tile].reshape(text_tile * requests, local_cols)
    image_att = attended[text_tile:].reshape(image_count * requests, local_cols)
    image_term = jnp.dot(image_att, proj_image, preferred_element_type=jnp.float32).reshape(
        image_count, requests, model_width
    )
    image_sum = sum_over_tensor(image_term, owners, NARROW_SUMS)
    text_term = jnp.dot(text_att, proj_text, preferred_element_type=jnp.float32).reshape(
        text_tile, requests, model_width
    )
    after_image = (image_sum[0, 0, 0] * 0.0).astype(text_term.dtype)
    text_sum = sum_over_tensor(text_term + after_image, owners, NARROW_SUMS)
    image_mid = (image_own.astype(jnp.float32) + mod_image[None, :, 2, :] * image_sum).astype(
        jnp.bfloat16
    )
    mlp_mod = modulate(image_mid, mod_mlp[None, :, 0, :], mod_mlp[None, :, 1, :])
    piece = lax.all_gather(mlp_mod, "tensor", axis=0, tiled=True)
    grown = jnp.dot(piece.reshape(-1, model_width), mlp_expand, preferred_element_type=jnp.float32)
    activated = jax.nn.gelu(grown, approximate=True).astype(jnp.bfloat16)
    text_out = (text_own.astype(jnp.float32) + mod_text[None, :, 2, :] * text_sum).astype(
        jnp.bfloat16
    )
    mlp_term = jnp.dot(activated, mlp_reduce, preferred_element_type=jnp.float32).reshape(
        image_count, requests, model_width
    )
    mlp_sum = sum_over_tensor(mlp_term, owners, NARROW_SUMS)
    image_out = (image_mid.astype(jnp.float32) + mod_mlp[None, :, 2, :] * mlp_sum).astype(
        jnp.bfloat16
    )
    final_in = modulate(image_out, mod_final[None, :, 0, :], mod_final[None, :, 1, :])
    velocity = jnp.dot(
        final_in.reshape(own_image * requests, model_width),
        final_weight,
        preferred_element_type=jnp.float32,
    ).reshape(own_image, requests, final_weight.shape[1])
    velocity = velocity.transpose(1, 0, 2).reshape(
        requests, tile_rows, tile_cols * final_weight.shape[1]
    )
    step_float = step_index.astype(jnp.float32)
    time_delta = sigma_of(step_float + 1.0) - sigma_of(step_float)
    latents_next = latents + time_delta[:, None, None] * velocity
    latents_ext = padded(latents_next, (("tile", 1),), 1)
    image_out = image_out.transpose(1, 0, 2).reshape(requests, tile_rows, tile_cols, model_width)
    return (image_out, text_out.transpose(1, 0, 2), latents_ext)


def solution(mesh):
    return jax.shard_map(
        per_device,
        mesh=mesh,
        in_specs=(
            P(None, "tile", "tensor", None),
            P(None, ("tile", "tensor"), None),
            P(None, "tile", "tensor"),
            P(),
            P(),
            P(),
            P(),
            P(),
            P(),
            P(),
            P(None, None, "tensor"),
            P(None, None, "tensor"),
            P("tensor", None),
            P("tensor", None),
            P(),
            P(None, "tensor"),
            P("tensor", None),
            P(),
        ),
        out_specs=(
            P(None, "tile", "tensor", None),
            P(None, ("tile", "tensor"), None),
            P(None, "tile", "tensor"),
        ),
        check_vma=False,
    )
```

```python
import math

import jax
import jax.numpy as jnp
from jax import lax
from jax.sharding import PartitionSpec as P

HEAD_DIM = 128
GRID = 32
NSTEPS = 28


norm_eps = 1e-06
time_shift = 3.0


def padded(value, sides, width):
    for axis, dim in sides:
        size, length = (lax.axis_size(axis), value.shape[dim])
        up = [(i, (i + 1) % size) for i in range(size - 1)]
        down = [(j, i) for i, j in up]
        last = lax.slice_in_dim(value, length - width, length, axis=dim)
        leading = lax.slice_in_dim(value, 0, width, axis=dim)
        before = lax.ppermute(last, axis, up)
        after = lax.ppermute(leading, axis, down)
        value = jnp.concatenate([before, value, after], axis=dim)
    return value


def layer_norm(values):
    average = jnp.mean(values, -1, keepdims=True)
    centred = values - average
    spread = jnp.mean(centred * centred, -1, keepdims=True)
    return centred * lax.rsqrt(spread + norm_eps)


def modulate(hidden, shift, stretch):
    normed = layer_norm(hidden.astype(jnp.float32))
    return ((1.0 + stretch) * normed + shift).astype(jnp.bfloat16)


def rope_tables(row_ids, col_ids):
    lane = jnp.arange(2 * 64, dtype=jnp.int32)
    pair_index = lane // 2
    row_rank = (pair_index - 8).astype(jnp.float32)
    col_rank = (pair_index - 36).astype(jnp.float32)
    log_base = math.log(10000.0)
    row_freq = jnp.where(
        (pair_index >= 8) & (pair_index < 36), jnp.exp(-2.0 * row_rank / 56.0 * log_base), 0.0
    )
    col_freq = jnp.where(pair_index >= 36, jnp.exp(-2.0 * col_rank / 56.0 * log_base), 0.0)
    angles = row_ids[..., None] * row_freq + col_ids[..., None] * col_freq
    sign_table = jnp.where(lane % 2 == 0, -1.0, 1.0).astype(jnp.float32)
    return (jnp.cos(angles), jnp.sin(angles) * sign_table)


def rotate(values, cos_table, sin_table):
    lane = lax.broadcasted_iota(jnp.int32, values.shape, values.ndim - 1)
    swapped = jnp.where(
        lane % 2 == 0, jnp.roll(values, -1, axis=-1), jnp.roll(values, 1, axis=-1)
    )
    return values * cos_table + swapped * sin_table


def head_norm(projected, head_gain):
    squares = jnp.mean(projected * projected, -1, keepdims=True)
    return projected * lax.rsqrt(squares + norm_eps) * head_gain


def sigma_of(step_float):
    level = 1.0 - step_float / NSTEPS
    return time_shift * level / (1.0 + (time_shift - 1.0) * level)


def key_usable(text_len, key_count, text_tile, block_len):
    key_pos = jnp.arange(key_count, dtype=jnp.int32)
    owner_tile = key_pos // block_len
    offset = key_pos % block_len
    text_pos = owner_tile * text_tile + offset
    return jnp.logical_or(offset[None, :] >= text_tile, text_pos[None, :] < text_len[:, None])


def sum_over_tensor(term, owners, narrow):
    if not narrow:
        return lax.psum_scatter(term, "tensor", scatter_dimension=0, tiled=True)
    parts = term.astype(jnp.bfloat16).reshape((owners, -1) + term.shape[1:])
    parts = lax.all_to_all(parts, "tensor", 0, 0, tiled=True)
    return jnp.sum(parts.astype(jnp.float32), 0)


NARROW_SUMS = True


def per_device(
    image_hidden,
    text_hidden,
    latents,
    step_index,
    anchor,
    text_len,
    mod_image,
    mod_text,
    mod_mlp,
    mod_final,
    qkv_image,
    qkv_text,
    proj_image,
    proj_text,
    qk_gain,
    mlp_expand,
    mlp_reduce,
    final_weight,
):
    requests, tile_rows, tile_cols, model_width = image_hidden.shape
    local_cols = qkv_image.shape[2]
    local_heads = local_cols // HEAD_DIM
    owners = lax.axis_size("tensor")
    own_image = tile_rows * tile_cols
    own_text = text_hidden.shape[1]
    slots = own_image + own_text
    image_own = image_hidden.reshape(requests, own_image, model_width).transpose(1, 0, 2)
    text_own = text_hidden.transpose(1, 0, 2)
    image_mod_own = modulate(image_own, mod_image[None, :, 0, :], mod_image[None, :, 1, :])
    text_mod_own = modulate(text_own, mod_text[None, :, 0, :], mod_text[None, :, 1, :])
    image_count = owners * own_image
    text_tile = owners * own_text
    block_len = text_tile + image_count
    image_mod = lax.all_gather(image_mod_own, "tensor", axis=0, tiled=True).reshape(
        image_count * requests, model_width
    )
    text_mod = lax.all_to_all(
        jnp.broadcast_to(text_mod_own[None], (owners,) + text_mod_own.shape), "tensor", 0, 0,
        tiled=True,
    ).reshape(text_tile * requests, model_width)
    tile_index = lax.axis_index("tile")
    token_index = jnp.arange(image_count, dtype=jnp.int32)
    owner = token_index // own_image
    within = token_index % own_image
    row_ids = (anchor[None, :, 0] + tile_index * tile_rows + (within // tile_cols)[:, None]).astype(
        jnp.float32
    )
    col_ids = (anchor[None, :, 1] + (owner * tile_cols + within % tile_cols)[:, None]).astype(
        jnp.float32
    )
    cos_table, sin_table = rope_tables(row_ids, col_ids)
    cos_table = cos_table[:, :, None, :]
    sin_table = sin_table[:, :, None, :]
    image_qkv = jnp.dot(
        image_mod, qkv_image.reshape(model_width, 3 * local_cols), preferred_element_type=jnp.float32
    ).reshape(image_count, requests, 3, local_heads, HEAD_DIM)
    text_qkv = jnp.dot(
        text_mod, qkv_text.reshape(model_width, 3 * local_cols), preferred_element_type=jnp.float32
    ).reshape(text_tile, requests, 3, local_heads, HEAD_DIM)
    query = jnp.concatenate(
        [
            head_norm(text_qkv[:, :, 0], qk_gain[1, 0]).astype(jnp.bfloat16),
            rotate(head_norm(image_qkv[:, :, 0], qk_gain[0, 0]), cos_table, sin_table).astype(
                jnp.bfloat16
            ),
        ],
        0,
    )
    keys = jnp.concatenate(
        [
            head_norm(text_qkv[:, :, 1], qk_gain[1, 1]).astype(jnp.bfloat16),
            rotate(head_norm(image_qkv[:, :, 1], qk_gain[0, 1]), cos_table, sin_table).astype(
                jnp.bfloat16
            ),
        ],
        0,
    )
    values = jnp.concatenate([text_qkv[:, :, 2], image_qkv[:, :, 2]], 0).astype(jnp.bfloat16)
    score_scale = 1.0 / math.sqrt(HEAD_DIM)
    tiles = lax.axis_size("tile")
    parts = tiles // requests
    part_len = block_len // parts
    keys_r = jnp.repeat(keys.transpose(1, 0, 2, 3), parts, axis=0)
    values_r = jnp.repeat(values.transpose(1, 0, 2, 3), parts, axis=0)
    query_r = query.transpose(1, 0, 2, 3).reshape(tiles, part_len, local_heads, HEAD_DIM)
    outgoing = jnp.concatenate([keys_r, values_r, query_r], 1)
    incoming = lax.all_to_all(outgoing, "tile", 0, 0, tiled=True)
    keys_all = incoming[:, :block_len].reshape(tiles * block_len, local_heads, HEAD_DIM)
    values_all = incoming[:, block_len : 2 * block_len].reshape(
        tiles * block_len, local_heads, HEAD_DIM
    )
    query_mine = incoming[:, 2 * block_len :].reshape(tiles * part_len, local_heads, HEAD_DIM)
    my_request = tile_index // parts
    usable = key_usable(text_len[my_request][None], keys_all.shape[0], text_tile, block_len)[
        0
    ][None, None, :]
    scores = (
        jnp.einsum("qhd,khd->hqk", query_mine, keys_all, preferred_element_type=jnp.float32)
        * score_scale
    )
    row_top = jnp.max(jnp.where(usable, scores, -jnp.inf), -1, keepdims=True)
    weights_raw = jnp.where(usable, jnp.exp(scores - row_top), 0.0)
    weight_sum = jnp.sum(weights_raw, -1, keepdims=True)
    accum = jnp.einsum(
        "hqk,khd->hqd",
        weights_raw.astype(jnp.bfloat16),
        values_all,
        preferred_element_type=jnp.float32,
    )
    attended_mine = (
        (accum / weight_sum).astype(jnp.bfloat16).transpose(1, 0, 2).reshape(
            tiles, part_len, local_heads * HEAD_DIM
        )
    )
    returned = lax.all_to_all(attended_mine, "tile", 0, 0, tiled=True)
    attended = returned.reshape(requests, block_len, local_cols).transpose(1, 0, 2)
    text_att = attended[:text_tile].reshape(text_tile * requests, local_cols)
    image_att = attended[text_tile:].reshape(image_count * requests, local_cols)
    image_term = jnp.dot(image_att, proj_image, preferred_element_type=jnp.float32).reshape(
        image_count, requests, model_width
    )
    image_sum = sum_over_tensor(image_term, owners, NARROW_SUMS)
    text_term = jnp.dot(text_att, proj_text, preferred_element_type=jnp.float32).reshape(
        text_tile, requests, model_width
    )
    image_mid = (image_own.astype(jnp.float32) + mod_image[None, :, 2, :] * image_sum).astype(
        jnp.bfloat16
    )
    mlp_mod = modulate(image_mid, mod_mlp[None, :, 0, :], mod_mlp[None, :, 1, :])
    piece = lax.all_gather(mlp_mod, "tensor", axis=0, tiled=True)
    grown = jnp.dot(piece.reshape(-1, model_width), mlp_expand, preferred_element_type=jnp.float32)
    activated = jax.nn.gelu(grown, approximate=True).astype(jnp.bfloat16)
    mlp_term = jnp.dot(activated, mlp_reduce, preferred_element_type=jnp.float32).reshape(
        image_count, requests, model_width
    )
    mlp_sum = sum_over_tensor(mlp_term, owners, NARROW_SUMS)
    after_mlp = (mlp_sum[0, 0, 0] * 0.0).astype(text_term.dtype)
    text_sum = sum_over_tensor(text_term + after_mlp, owners, NARROW_SUMS)
    text_out = (text_own.astype(jnp.float32) + mod_text[None, :, 2, :] * text_sum).astype(
        jnp.bfloat16
    )
    image_out = (image_mid.astype(jnp.float32) + mod_mlp[None, :, 2, :] * mlp_sum).astype(
        jnp.bfloat16
    )
    final_in = modulate(image_out, mod_final[None, :, 0, :], mod_final[None, :, 1, :])
    velocity = jnp.dot(
        final_in.reshape(own_image * requests, model_width),
        final_weight,
        preferred_element_type=jnp.float32,
    ).reshape(own_image, requests, final_weight.shape[1])
    velocity = velocity.transpose(1, 0, 2).reshape(
        requests, tile_rows, tile_cols * final_weight.shape[1]
    )
    step_float = step_index.astype(jnp.float32)
    time_delta = sigma_of(step_float + 1.0) - sigma_of(step_float)
    latents_next = latents + time_delta[:, None, None] * velocity
    latents_ext = padded(latents_next, (("tile", 1),), 1)
    image_out = image_out.transpose(1, 0, 2).reshape(requests, tile_rows, tile_cols, model_width)
    return (image_out, text_out.transpose(1, 0, 2), latents_ext)


def solution(mesh):
    return jax.shard_map(
        per_device,
        mesh=mesh,
        in_specs=(
            P(None, "tile", "tensor", None),
            P(None, ("tile", "tensor"), None),
            P(None, "tile", "tensor"),
            P(),
            P(),
            P(),
            P(),
            P(),
            P(),
            P(),
            P(None, None, "tensor"),
            P(None, None, "tensor"),
            P("tensor", None),
            P("tensor", None),
            P(),
            P(None, "tensor"),
            P("tensor", None),
            P(),
        ),
        out_specs=(
            P(None, "tile", "tensor", None),
            P(None, ("tile", "tensor"), None),
            P(None, "tile", "tensor"),
        ),
        check_vma=False,
    )
```

```python
import math

import jax
import jax.numpy as jnp
from jax import lax
from jax.sharding import PartitionSpec as P

HEAD_DIM = 128
GRID = 32
NSTEPS = 28


norm_eps = 1e-06
time_shift = 3.0


def padded(value, sides, width):
    for axis, dim in sides:
        size, length = (lax.axis_size(axis), value.shape[dim])
        up = [(i, (i + 1) % size) for i in range(size - 1)]
        down = [(j, i) for i, j in up]
        last = lax.slice_in_dim(value, length - width, length, axis=dim)
        leading = lax.slice_in_dim(value, 0, width, axis=dim)
        before = lax.ppermute(last, axis, up)
        after = lax.ppermute(leading, axis, down)
        value = jnp.concatenate([before, value, after], axis=dim)
    return value


def layer_norm(values):
    average = jnp.mean(values, -1, keepdims=True)
    centred = values - average
    spread = jnp.mean(centred * centred, -1, keepdims=True)
    return centred * lax.rsqrt(spread + norm_eps)


def modulate(hidden, shift, stretch):
    normed = layer_norm(hidden.astype(jnp.float32))
    return ((1.0 + stretch) * normed + shift).astype(jnp.bfloat16)


def rope_tables(row_ids, col_ids):
    lane = jnp.arange(2 * 64, dtype=jnp.int32)
    pair_index = lane // 2
    row_rank = (pair_index - 8).astype(jnp.float32)
    col_rank = (pair_index - 36).astype(jnp.float32)
    log_base = math.log(10000.0)
    row_freq = jnp.where(
        (pair_index >= 8) & (pair_index < 36), jnp.exp(-2.0 * row_rank / 56.0 * log_base), 0.0
    )
    col_freq = jnp.where(pair_index >= 36, jnp.exp(-2.0 * col_rank / 56.0 * log_base), 0.0)
    angles = row_ids[..., None] * row_freq + col_ids[..., None] * col_freq
    sign_table = jnp.where(lane % 2 == 0, -1.0, 1.0).astype(jnp.float32)
    return (jnp.cos(angles), jnp.sin(angles) * sign_table)


def rotate(values, cos_table, sin_table):
    lane = lax.broadcasted_iota(jnp.int32, values.shape, values.ndim - 1)
    swapped = jnp.where(
        lane % 2 == 0, jnp.roll(values, -1, axis=-1), jnp.roll(values, 1, axis=-1)
    )
    return values * cos_table + swapped * sin_table


def head_norm(projected, head_gain):
    squares = jnp.mean(projected * projected, -1, keepdims=True)
    return projected * lax.rsqrt(squares + norm_eps) * head_gain


def sigma_of(step_float):
    level = 1.0 - step_float / NSTEPS
    return time_shift * level / (1.0 + (time_shift - 1.0) * level)


def key_usable(text_len, key_count, text_tile, block_len):
    key_pos = jnp.arange(key_count, dtype=jnp.int32)
    owner_tile = key_pos // block_len
    offset = key_pos % block_len
    text_pos = owner_tile * text_tile + offset
    return jnp.logical_or(offset[None, :] >= text_tile, text_pos[None, :] < text_len[:, None])


def sum_over_tensor(term, owners, narrow):
    if not narrow:
        return lax.psum_scatter(term, "tensor", scatter_dimension=0, tiled=True)
    parts = term.astype(jnp.bfloat16).reshape((owners, -1) + term.shape[1:])
    parts = lax.all_to_all(parts, "tensor", 0, 0, tiled=True)
    return jnp.sum(parts.astype(jnp.float32), 0)


NARROW_SUMS = True


def per_device(
    image_hidden,
    text_hidden,
    latents,
    step_index,
    anchor,
    text_len,
    mod_image,
    mod_text,
    mod_mlp,
    mod_final,
    qkv_image,
    qkv_text,
    proj_image,
    proj_text,
    qk_gain,
    mlp_expand,
    mlp_reduce,
    final_weight,
):
    requests, tile_rows, tile_cols, model_width = image_hidden.shape
    local_cols = qkv_image.shape[2]
    local_heads = local_cols // HEAD_DIM
    owners = lax.axis_size("tensor")
    own_image = tile_rows * tile_cols
    own_text = text_hidden.shape[1]
    slots = own_image + own_text
    image_own = image_hidden.reshape(requests, own_image, model_width).transpose(1, 0, 2)
    text_own = text_hidden.transpose(1, 0, 2)
    image_mod_own = modulate(image_own, mod_image[None, :, 0, :], mod_image[None, :, 1, :])
    text_mod_own = modulate(text_own, mod_text[None, :, 0, :], mod_text[None, :, 1, :])
    image_count = owners * own_image
    text_tile = owners * own_text
    block_len = text_tile + image_count
    image_mod = lax.all_gather(image_mod_own, "tensor", axis=0, tiled=True).reshape(
        image_count * requests, model_width
    )
    text_mod = lax.all_to_all(
        jnp.broadcast_to(text_mod_own[None], (owners,) + text_mod_own.shape), "tensor", 0, 0,
        tiled=True,
    ).reshape(text_tile * requests, model_width)
    tile_index = lax.axis_index("tile")
    token_index = jnp.arange(image_count, dtype=jnp.int32)
    owner = token_index // own_image
    within = token_index % own_image
    row_ids = (anchor[None, :, 0] + tile_index * tile_rows + (within // tile_cols)[:, None]).astype(
        jnp.float32
    )
    col_ids = (anchor[None, :, 1] + (owner * tile_cols + within % tile_cols)[:, None]).astype(
        jnp.float32
    )
    cos_table, sin_table = rope_tables(row_ids.reshape(-1), col_ids.reshape(-1))
    cos_table = cos_table[:, None, :]
    sin_table = sin_table[:, None, :]
    image_qkv = jnp.dot(
        image_mod, qkv_image.reshape(model_width, 3 * local_cols), preferred_element_type=jnp.float32
    ).reshape(image_count * requests, 3, local_heads, HEAD_DIM)
    text_qkv = jnp.dot(
        text_mod, qkv_text.reshape(model_width, 3 * local_cols), preferred_element_type=jnp.float32
    ).reshape(text_tile * requests, 3, local_heads, HEAD_DIM)
    token_shape = (block_len, requests, local_heads, HEAD_DIM)
    query = jnp.concatenate(
        [
            head_norm(text_qkv[:, 0], qk_gain[1, 0]).astype(jnp.bfloat16),
            rotate(head_norm(image_qkv[:, 0], qk_gain[0, 0]), cos_table, sin_table).astype(
                jnp.bfloat16
            ),
        ],
        0,
    ).reshape(token_shape)
    keys = jnp.concatenate(
        [
            head_norm(text_qkv[:, 1], qk_gain[1, 1]).astype(jnp.bfloat16),
            rotate(head_norm(image_qkv[:, 1], qk_gain[0, 1]), cos_table, sin_table).astype(
                jnp.bfloat16
            ),
        ],
        0,
    ).reshape(token_shape)
    values = (
        jnp.concatenate([text_qkv[:, 2], image_qkv[:, 2]], 0).astype(jnp.bfloat16).reshape(token_shape)
    )
    score_scale = 1.0 / math.sqrt(HEAD_DIM)
    tiles = lax.axis_size("tile")
    parts = tiles // requests
    part_len = block_len // parts
    keys_r = jnp.repeat(keys.transpose(1, 0, 2, 3), parts, axis=0)
    values_r = jnp.repeat(values.transpose(1, 0, 2, 3), parts, axis=0)
    query_r = query.transpose(1, 0, 2, 3).reshape(tiles, part_len, local_heads, HEAD_DIM)
    outgoing = jnp.concatenate([keys_r, values_r, query_r], 1)
    incoming = lax.all_to_all(outgoing, "tile", 0, 0, tiled=True)
    keys_all = incoming[:, :block_len].reshape(tiles * block_len, local_heads, HEAD_DIM)
    values_all = incoming[:, block_len : 2 * block_len].reshape(
        tiles * block_len, local_heads, HEAD_DIM
    )
    query_mine = incoming[:, 2 * block_len :].reshape(tiles * part_len, local_heads, HEAD_DIM)
    my_request = tile_index // parts
    usable = key_usable(text_len[my_request][None], keys_all.shape[0], text_tile, block_len)[
        0
    ][None, None, :]
    scores = (
        jnp.einsum("qhd,khd->hqk", query_mine, keys_all, preferred_element_type=jnp.float32)
        * score_scale
    )
    row_top = jnp.max(jnp.where(usable, scores, -jnp.inf), -1, keepdims=True)
    weights_raw = jnp.where(usable, jnp.exp(scores - row_top), 0.0)
    weight_sum = jnp.sum(weights_raw, -1, keepdims=True)
    accum = jnp.einsum(
        "hqk,khd->hqd",
        weights_raw.astype(jnp.bfloat16),
        values_all,
        preferred_element_type=jnp.float32,
    )
    attended_mine = (
        (accum / weight_sum).astype(jnp.bfloat16).transpose(1, 0, 2).reshape(
            tiles, part_len, local_heads * HEAD_DIM
        )
    )
    returned = lax.all_to_all(attended_mine, "tile", 0, 0, tiled=True)
    attended = returned.reshape(requests, block_len, local_cols).transpose(1, 0, 2)
    text_att = attended[:text_tile].reshape(text_tile * requests, local_cols)
    image_att = attended[text_tile:].reshape(image_count * requests, local_cols)
    image_term = jnp.dot(image_att, proj_image, preferred_element_type=jnp.float32).reshape(
        image_count, requests, model_width
    )
    image_sum = sum_over_tensor(image_term, owners, NARROW_SUMS)
    text_term = jnp.dot(text_att, proj_text, preferred_element_type=jnp.float32).reshape(
        text_tile, requests, model_width
    )
    after_image = (image_sum[0, 0, 0] * 0.0).astype(text_term.dtype)
    text_sum = sum_over_tensor(text_term + after_image, owners, NARROW_SUMS)
    image_mid = (image_own.astype(jnp.float32) + mod_image[None, :, 2, :] * image_sum).astype(
        jnp.bfloat16
    )
    mlp_mod = modulate(image_mid, mod_mlp[None, :, 0, :], mod_mlp[None, :, 1, :])
    piece = lax.all_gather(mlp_mod, "tensor", axis=0, tiled=True)
    grown = jnp.dot(piece.reshape(-1, model_width), mlp_expand, preferred_element_type=jnp.float32)
    activated = jax.nn.gelu(grown, approximate=True).astype(jnp.bfloat16)
    text_out = (text_own.astype(jnp.float32) + mod_text[None, :, 2, :] * text_sum).astype(
        jnp.bfloat16
    )
    mlp_term = jnp.dot(activated, mlp_reduce, preferred_element_type=jnp.float32).reshape(
        image_count, requests, model_width
    )
    mlp_sum = sum_over_tensor(mlp_term, owners, NARROW_SUMS)
    image_out = (image_mid.astype(jnp.float32) + mod_mlp[None, :, 2, :] * mlp_sum).astype(
        jnp.bfloat16
    )
    final_in = modulate(image_out, mod_final[None, :, 0, :], mod_final[None, :, 1, :])
    velocity = jnp.dot(
        final_in.reshape(own_image * requests, model_width),
        final_weight,
        preferred_element_type=jnp.float32,
    ).reshape(own_image, requests, final_weight.shape[1])
    velocity = velocity.transpose(1, 0, 2).reshape(
        requests, tile_rows, tile_cols * final_weight.shape[1]
    )
    step_float = step_index.astype(jnp.float32)
    time_delta = sigma_of(step_float + 1.0) - sigma_of(step_float)
    latents_next = latents + time_delta[:, None, None] * velocity
    latents_ext = padded(latents_next, (("tile", 1),), 1)
    image_out = image_out.transpose(1, 0, 2).reshape(requests, tile_rows, tile_cols, model_width)
    return (image_out, text_out.transpose(1, 0, 2), latents_ext)


def solution(mesh):
    return jax.shard_map(
        per_device,
        mesh=mesh,
        in_specs=(
            P(None, "tile", "tensor", None),
            P(None, ("tile", "tensor"), None),
            P(None, "tile", "tensor"),
            P(),
            P(),
            P(),
            P(),
            P(),
            P(),
            P(),
            P(None, None, "tensor"),
            P(None, None, "tensor"),
            P("tensor", None),
            P("tensor", None),
            P(),
            P(None, "tensor"),
            P("tensor", None),
            P(),
        ),
        out_specs=(
            P(None, "tile", "tensor", None),
            P(None, ("tile", "tensor"), None),
            P(None, "tile", "tensor"),
        ),
        check_vma=False,
    )
```
